128 devices in a mesh: depth: 4 (over z_lo, core), lat: 32 (over y, z_hi, x).
Axes of the slice: x: 4, y: 4, z: 4 (z_hi: 2, z_lo: 2; z = z_hi * 2 + z_lo), core: 2. Of those that a mesh axis runs over, the one named last changes fastest.
Arguments:
- temp_old: float32 [32, 32, 256, 128], P('depth', 'lat'), may hold values from 0 to 2.5
- material: int32 [32, 32, 256, 128], P('depth', 'lat'), may hold values from 0 to 7
- conduct_table: float32 [8], replicated, may hold values from 0.3 to 3
- capacity_table: float32 [8], replicated, may hold values from 0.5 to 2
- dyn_power: float32 [4, 32, 256, 128], P('depth', 'lat'), may hold values from 0.2 to 4
- leak_ref: float32 [4, 32, 256, 128], P('depth', 'lat'), may hold values from 0.05 to 1
- die_layer: int32 [4], replicated, may hold values from 0 to 31, as said below
Outputs:
- temp_new: float32 [32, 32, 256, 128], P('depth', 'lat')
- die_power: float32 [4, 32, 256, 128], P('depth', 'lat')
The draws below stay inside these ranges and needn't reach their ends.
Inputs may be any that keep to these rules, and one draw needn't show every extreme that they name: `die_layer`: the 4 entries name different layers of the grid; one die lies on layer 0 and one on the top layer.
All inputs are finite; a program needn't handle non-finite values.
Results may differ from the reference program's by a relative error of at most 0.000059.
Values sent between devices are 32-bit elements; how exact they have to be, the bound alone decides.
No kernel may reach another device: no remote copies, remote signals or barrier semaphores. Data moves between devices by JAX's collectives and lax.ppermute only.
A program may use at most 128 MiB of HBM per device.

```python
import math
import jax
import jax.numpy as jnp

BX = 256
BY = 128
GX = 1
DIES = 4
MATS = 8
SWEEPS = 6
TILES = 32
GY = 32
NZ = 32


def draw_die_layer(key, part):
    middle = jax.random.permutation(jax.random.fold_in(key, 11), NZ - 2)[:DIES - 2] + 1
    ends = jnp.array([0, NZ - 1], dtype=jnp.int32)
    layers = jnp.concatenate([ends, middle.astype(jnp.int32)])
    order = jax.random.permutation(jax.random.fold_in(key, 23), DIES)
    return layers[order].astype(jnp.int32)


def via_material(key):
    return jax.random.randint(jax.random.fold_in(key, 5), (), 0, MATS).astype(jnp.int32)


def draw_material(key, part):
    chosen = via_material(key)
    base = jax.random.randint(jax.random.fold_in(key, 7), (NZ, TILES, BX, BY), 0, MATS - 1).astype(jnp.int32)
    base = base + (base >= chosen).astype(jnp.int32)
    column = jax.random.randint(jax.random.fold_in(key, 13), (1, TILES, BX, BY), 0, 8) == 0
    wiring = jax.random.randint(jax.random.fold_in(key, 17), (NZ, 1, BX, 1), 0, 8) == 0
    marked = jnp.logical_or(column, wiring)
    return jnp.where(marked, chosen, base).astype(jnp.int32)


def draw_conduct_table(key, part):
    chosen = via_material(key)
    entries = jnp.arange(MATS, dtype=jnp.int32)
    spread = jax.random.uniform(jax.random.fold_in(key, 31), (MATS,), jnp.float32)
    low_value = 0.3 * jnp.exp(jnp.log(10.0 / 3.0) * spread)
    high_value = 2.4 + 0.6 * spread
    return jnp.where(entries == chosen, high_value, low_value).astype(jnp.float32)


def levels(own_key, extent, split, low, high):
    factor_of, own = 1.0, jax.random.fold_in(own_key, 6)
    for axis_at, parts in split:
        draws = jnp.exp(jax.random.uniform(jax.random.fold_in(own, axis_at), (parts,), jnp.float32, low / len(split), high / len(split)))
        factor_of = factor_of * jnp.repeat(draws, extent[axis_at] // parts).reshape([-1 if axis == axis_at else 1 for axis in range(len(extent))])
    return factor_of


def setup_inputs(seed: int = 0) -> dict:
    streams_of = jax.random.split(jax.random.key(seed), 8)
    return {
        "temp_old": jnp.clip(2.5 * jax.random.uniform(streams_of[0], (NZ, TILES, BX, BY), jnp.float32) ** levels(streams_of[0], (NZ, TILES, BX, BY), ((0, 4), (1, 32)), -0.2, 0.2), 0.0, 2.5),
        "material": draw_material(jax.random.fold_in(streams_of[7], 71), 0),
        "conduct_table": draw_conduct_table(jax.random.fold_in(streams_of[7], 71), 0),
        "capacity_table": jnp.clip(jnp.exp(jax.random.uniform(streams_of[3], (MATS,), jnp.float32, math.log(0.5), math.log(2.0))), 0.5, 2.0),
        "dyn_power": jnp.clip(jnp.exp(math.log(4.0) - 2.9957323 * jax.random.uniform(streams_of[4], (DIES, TILES, BX, BY), jnp.float32) ** levels(streams_of[4], (DIES, TILES, BX, BY), ((0, 4), (1, 32)), -0.2, 0.2)), 0.2, 4.0),
        "leak_ref": jnp.clip(jnp.exp(math.log(1.0) - 2.9957323 * jax.random.uniform(streams_of[5], (DIES, TILES, BX, BY), jnp.float32) ** levels(streams_of[5], (DIES, TILES, BX, BY), ((0, 4), (1, 32)), -0.2, 0.2)), 0.05, 1.0),
        "die_layer": draw_die_layer(jax.random.fold_in(streams_of[7], 71), 0),
    }


COND_SLOPE = 0.15
LEAK_SLOPE = 0.5
SINK_CONDUCT = 2.0


def harmonic(first_side, second_side):
    return 2.0 * first_side * second_side / (first_side + second_side)


def to_grid(tiled):
    leading = tiled.shape[0]
    shaped = tiled.reshape(leading, GX, GY, BX, BY)
    return jnp.transpose(shaped, (0, 1, 3, 2, 4)).reshape(leading, GX * BX, GY * BY)


def to_tiles(grid):
    leading = grid.shape[0]
    shaped = grid.reshape(leading, GX, BX, GY, BY)
    return jnp.transpose(shaped, (0, 1, 3, 2, 4)).reshape(leading, GX * GY, BX, BY)


def reference(temp_old, material, conduct_table, capacity_table, dyn_power, leak_ref, die_layer):
    temp_grid = to_grid(temp_old)
    mat_grid = to_grid(material)
    die_temp = temp_grid[die_layer]
    die_power = to_grid(dyn_power) + to_grid(leak_ref) * jnp.exp(LEAK_SLOPE * die_temp)
    cond = conduct_table[mat_grid] * jnp.exp(-COND_SLOPE * temp_grid)
    heat_cap = capacity_table[mat_grid]
    source = jnp.zeros_like(temp_grid).at[die_layer].set(die_power)
    right_side = heat_cap * temp_grid + source
    along_z = jnp.pad(harmonic(cond[1:], cond[:-1]), ((1, 1), (0, 0), (0, 0)))
    along_x = jnp.pad(harmonic(cond[:, 1:], cond[:, :-1]), ((0, 0), (1, 1), (0, 0)))
    along_y = jnp.pad(harmonic(cond[:, :, 1:], cond[:, :, :-1]), ((0, 0), (0, 0), (1, 1)))
    layers = jnp.arange(NZ)[:, None, None]
    sink = jnp.where(layers == 0, SINK_CONDUCT, 0.0)
    diagonal = heat_cap + (along_z[1:] + along_z[:-1] + along_x[:, 1:] + along_x[:, :-1]
                           + along_y[:, :, 1:] + along_y[:, :, :-1]) + sink
    temp = temp_grid
    for sweep_index in range(SWEEPS):
        padded_z = jnp.pad(temp, ((1, 1), (0, 0), (0, 0)))
        padded_x = jnp.pad(temp, ((0, 0), (1, 1), (0, 0)))
        padded_y = jnp.pad(temp, ((0, 0), (0, 0), (1, 1)))
        coupled = (along_z[1:] * padded_z[2:] + along_z[:-1] * padded_z[:-2]
                   + along_x[:, 1:] * padded_x[:, 2:] + along_x[:, :-1] * padded_x[:, :-2]
                   + along_y[:, :, 1:] * padded_y[:, :, 2:] + along_y[:, :, :-1] * padded_y[:, :, :-2])
        temp = (right_side + coupled) / diagonal
    return to_tiles(temp), to_tiles(die_power)
```

```python
import functools

import jax
import jax.numpy as jnp
from jax import lax
from jax.experimental import pallas as pl
from jax.experimental.pallas import tpu as pltpu
from jax.sharding import PartitionSpec as P

SWEEPS = 6
HALO = SWEEPS
PAD_Y = 8

COND_SLOPE = 0.15
LEAK_SLOPE = 0.5
SINK_CONDUCT = 2.0

INTERPRET = False


def from_behind(block, axis, distance):
    devices = range(lax.axis_size(axis))
    route = [(i - distance, i) for i in devices if i - distance in devices]
    return lax.ppermute(block, axis, route)


def harm(a, b):
    summed = a + b
    return 2.0 * a * b / jnp.where(summed > 0, summed, 1.0)


def lookup(table_ref, material):
    looked = jnp.zeros(material.shape, jnp.float32)
    for entry in range(table_ref.shape[0]):
        looked = jnp.where(material == float(entry), table_ref[entry], looked)
    return looked


def sweep_kernel(nz, ny_total, local_depth, strip,
                 sc_ref, ctab_ref, htab_ref, xb_ref, xc_ref, xa_ref, dl_ref,
                 out_ref, t_s, cond_s, rhs_s, inv_s, gz_s, gx_s, gxl_s, gy_s, gyu_s):
    ze = t_s.shape[1]
    ye = t_s.shape[2]
    xe = t_s.shape[3]
    g = sc_ref[0]
    s = sc_ref[1]
    z0 = g * local_depth - HALO
    row = lax.broadcasted_iota(jnp.int32, (ye, xe), 0)
    lane = lax.broadcasted_iota(jnp.int32, (ye, xe), 1)
    yg = s * strip + row - PAD_Y
    yvalid = (yg >= 0) & (yg < ny_total) & (row >= PAD_Y - HALO) & (row < PAD_Y + strip + HALO)

    def tables(l, temp, mat):
        zg = z0 + l
        valid = yvalid & (zg >= 0) & (zg < nz)
        cval = lookup(ctab_ref, mat)
        hval = lookup(htab_ref, mat)
        cond = jnp.where(valid, cval * jnp.exp(-COND_SLOPE * temp), 0.0)
        t_s[0, l] = temp
        cond_s[l] = cond
        inv_s[l] = hval
        rhs_s[l] = hval * temp

    def below(i, c):
        tables(i, xb_ref[0, i], xb_ref[1, i])
        return c

    def centre(i, c):
        tables(HALO + i, xc_ref[0, i], xc_ref[1, i])
        return c

    def above(i, c):
        tables(HALO + local_depth + i, xa_ref[0, i], xa_ref[1, i])
        return c

    lax.fori_loop(0, HALO, below, 0)
    lax.fori_loop(0, local_depth, centre, 0)
    lax.fori_loop(0, HALO, above, 0)

    for d in range(dl_ref.shape[0]):
        rel = sc_ref[2 + d] - z0
        relc = jnp.clip(rel, 0, ze - 1)

        @pl.when((rel >= 0) & (rel < ze))
        def _():
            power = dl_ref[d, 0] + dl_ref[d, 1] * jnp.exp(LEAK_SLOPE * t_s[0, relc])
            rhs_s[relc] = inv_s[relc] * t_s[0, relc] + power

    def faces_z(l, c):
        gz_s[l] = harm(cond_s[l], cond_s[l + 1])
        return c

    lax.fori_loop(0, ze - 1, faces_z, 0)
    gz_s[ze - 1] = jnp.zeros((ye, xe), jnp.float32)

    def faces(l, c):
        cc = cond_s[l]
        gx = harm(cc, pltpu.roll(cc, xe - 1, 1))
        gx = jnp.where(lane == xe - 1, 0.0, gx)
        gy = harm(cc, pltpu.roll(cc, ye - 1, 0))
        gy = jnp.where(row == ye - 1, 0.0, gy)
        gxl = pltpu.roll(gx, 1, 1)
        gyu = pltpu.roll(gy, 1, 0)
        gx_s[l] = gx
        gxl_s[l] = gxl
        gy_s[l] = gy
        gyu_s[l] = gyu
        lm = jnp.maximum(l - 1, 0)
        gzm = jnp.where(l > 0, gz_s[lm], 0.0)
        sink = jnp.where(z0 + l == 0, SINK_CONDUCT, 0.0)
        diag = inv_s[l] + (gz_s[l] + gzm + gx + gxl + gy + gyu) + sink
        inv_s[l] = 1.0 / diag
        return c

    lax.fori_loop(0, ze, faces, 0)

    def relax(src, l):
        t = t_s[src, l]
        coupled = (gz_s[l] * t_s[src, l + 1] + gz_s[l - 1] * t_s[src, l - 1]
                   + gx_s[l] * pltpu.roll(t, xe - 1, 1) + gxl_s[l] * pltpu.roll(t, 1, 1)
                   + gy_s[l] * pltpu.roll(t, ye - 1, 0) + gyu_s[l] * pltpu.roll(t, 1, 0))
        return (rhs_s[l] + coupled) * inv_s[l]

    for k in range(1, SWEEPS):
        src, dst = (k - 1) % 2, k % 2

        def body(l, c, src=src, dst=dst):
            t_s[dst, l] = relax(src, l)
            return c

        lax.fori_loop(k, ze - k, body, 0)

    last = (SWEEPS - 1) % 2

    def final(i, c):
        new = relax(last, HALO + i)
        out_ref[i] = new[PAD_Y:PAD_Y + strip]
        return c

    lax.fori_loop(0, local_depth, final, 0)


def local(temp_old, material, conduct_table, capacity_table, dyn_power, leak_ref, die_layer):
    temp_start = temp_old[:, 0]
    cells_mat = material[:, 0]
    local_depth, nx, strip = temp_start.shape
    depth_n = lax.axis_size("depth")
    lat_n = lax.axis_size("lat")
    nz = local_depth * depth_n
    g = lax.axis_index("depth")
    s = lax.axis_index("lat")
    first_layer = g * local_depth
    layer_ids = first_layer + lax.iota(jnp.int32, local_depth)

    select = (die_layer[:, None] == layer_ids[None, :]).astype(jnp.float32)
    picked = jnp.einsum("dz,zxy->dxy", select, temp_start, precision=lax.Precision.HIGHEST)
    die_temp = lax.psum_scatter(picked, "depth", scatter_dimension=0, tiled=True)
    die_power = dyn_power[:, 0] + leak_ref[:, 0] * jnp.exp(LEAK_SLOPE * die_temp)

    tt = jnp.transpose(temp_start, (0, 2, 1))
    mt = jnp.transpose(cells_mat, (0, 2, 1)).astype(jnp.float32)
    dt = jnp.transpose(dyn_power[:, 0], (0, 2, 1))
    lt = jnp.transpose(leak_ref[:, 0], (0, 2, 1))
    fields = jnp.concatenate([tt, mt, dt, lt], axis=0)
    lo = from_behind(fields[:, strip - HALO:], "lat", 1)
    hi = from_behind(fields[:, :HALO], "lat", -1)
    nf = fields.shape[0]
    ye = PAD_Y + strip + HALO + (-(PAD_Y + strip + HALO)) % 8
    zpad_lo = jnp.zeros((nf, PAD_Y - HALO, nx), jnp.float32)
    zpad_hi = jnp.zeros((nf, ye - (PAD_Y + strip + HALO), nx), jnp.float32)
    wide = jnp.concatenate([zpad_lo, lo, fields, hi, zpad_hi], axis=1)
    tm = wide[:2 * local_depth].reshape(2, local_depth, ye, nx)
    dl = wide[2 * local_depth:].reshape(2, ye, nx)

    xb = from_behind(tm[:, local_depth - HALO:], "depth", 1)
    xa = from_behind(tm[:, :HALO], "depth", -1)
    dl_all = lax.all_gather(dl, "depth", axis=0, tiled=False)

    sc = jnp.concatenate([jnp.stack([g, s]).astype(jnp.int32), die_layer.astype(jnp.int32)])
    ze = local_depth + 2 * HALO
    smem = pl.BlockSpec(memory_space=pltpu.MemorySpace.SMEM)
    vmem = pl.BlockSpec(memory_space=pltpu.MemorySpace.VMEM)
    full = (ze, ye, nx)
    kern = functools.partial(sweep_kernel, nz, strip * lat_n, local_depth, strip)
    out = pl.pallas_call(
        kern,
        out_shape=jax.ShapeDtypeStruct((local_depth, strip, nx), jnp.float32),
        in_specs=[smem, smem, smem, vmem, vmem, vmem, vmem],
        out_specs=vmem,
        scratch_shapes=[pltpu.VMEM((2,) + full, jnp.float32)] + [pltpu.VMEM(full, jnp.float32)] * 8,
        compiler_params=pltpu.CompilerParams(vmem_limit_bytes=60 * 1024 * 1024),
        interpret=INTERPRET,
    )(sc, conduct_table, capacity_table, xb, tm, xa, dl_all)
    temp_new = jnp.transpose(out, (0, 2, 1))
    return (temp_new[:, None], die_power[:, None])


def solution(mesh):
    return jax.shard_map(
        local,
        mesh=mesh,
        in_specs=(
            P("depth", "lat", None, None),
            P("depth", "lat", None, None),
            P(),
            P(),
            P("depth", "lat", None, None),
            P("depth", "lat", None, None),
            P(),
        ),
        out_specs=(P("depth", "lat", None, None), P("depth", "lat", None, None)),
        check_vma=False,
    )
```

```python
import functools

import jax
import jax.numpy as jnp
from jax import lax
from jax.experimental import pallas as pl
from jax.experimental.pallas import tpu as pltpu
from jax.sharding import PartitionSpec as P

SWEEPS = 6
HALO = SWEEPS
PAD_Y = 8

COND_SLOPE = 0.15
LEAK_SLOPE = 0.5
SINK_CONDUCT = 2.0

INTERPRET = False


def from_behind(block, axis, distance):
    devices = range(lax.axis_size(axis))
    route = [(i - distance, i) for i in devices if i - distance in devices]
    return lax.ppermute(block, axis, route)


def harm(a, b):
    summed = a + b
    return 2.0 * a * b / jnp.where(summed > 0, summed, 1.0)


def lookup(table_ref, material):
    looked = jnp.zeros(material.shape, jnp.float32)
    for entry in range(table_ref.shape[0]):
        looked = jnp.where(material == float(entry), table_ref[entry], looked)
    return looked


def sweep_kernel(nz, ny_total, local_depth, strip,
                 sc_ref, ctab_ref, htab_ref, xc_ref, ylo_ref, yhi_ref, xb_ref, xa_ref,
                 cb_ref, ca_ref, dc_ref, dlo_ref, dhi_ref,
                 out_ref, t_s, cond_s, rhs_s, inv_s, gz_s, gx_s, gxl_s, gy_s, gyu_s, dl_s):
    ze = t_s.shape[1]
    ye = t_s.shape[2]
    xe = t_s.shape[3]
    g = sc_ref[0]
    s = sc_ref[1]
    z0 = g * local_depth - HALO
    row = lax.broadcasted_iota(jnp.int32, (ye, xe), 0)
    lane = lax.broadcasted_iota(jnp.int32, (ye, xe), 1)
    yg = s * strip + row - PAD_Y
    yvalid = (yg >= 0) & (yg < ny_total) & (row >= PAD_Y - HALO) & (row < PAD_Y + strip + HALO)
    top = PAD_Y + strip + HALO
    zlo = jnp.zeros((PAD_Y - HALO, xe), jnp.float32)
    zhi = jnp.zeros((ye - top, xe), jnp.float32)

    def put(dst, centre, lo, hi):
        dst[PAD_Y - HALO:PAD_Y] = lo
        dst[PAD_Y:PAD_Y + strip] = centre
        dst[PAD_Y + strip:top] = hi
        dst[0:PAD_Y - HALO] = zlo
        dst[top:ye] = zhi

    def tables(l, parts):
        for f, dst in ((0, t_s.at[0, l]), (1, cond_s.at[l])):
            put(dst, *parts[f])
        temp = t_s[0, l]
        mat = cond_s[l]
        zg = z0 + l
        valid = yvalid & (zg >= 0) & (zg < nz)
        cval = lookup(ctab_ref, mat)
        hval = lookup(htab_ref, mat)
        cond = jnp.where(valid, cval * jnp.exp(-COND_SLOPE * temp), 0.0)
        cond_s[l] = cond
        inv_s[l] = hval
        rhs_s[l] = hval * temp

    def below(i, c):
        tables(i, [(xb_ref[f, i], cb_ref[f, i, :HALO], cb_ref[f, i, HALO:]) for f in range(2)])
        return c

    def centre(i, c):
        tables(HALO + i, [(xc_ref[f, i], ylo_ref[f * local_depth + i], yhi_ref[f * local_depth + i])
                          for f in range(2)])
        return c

    def above(i, c):
        tables(HALO + local_depth + i,
               [(xa_ref[f, i], ca_ref[f, i, :HALO], ca_ref[f, i, HALO:]) for f in range(2)])
        return c

    lax.fori_loop(0, HALO, below, 0)
    lax.fori_loop(0, local_depth, centre, 0)
    lax.fori_loop(0, HALO, above, 0)

    for d in range(dc_ref.shape[0]):
        rel = sc_ref[2 + d] - z0
        relc = jnp.clip(rel, 0, ze - 1)

        @pl.when((rel >= 0) & (rel < ze))
        def _():
            for f in range(2):
                put(dl_s.at[f], dc_ref[d, f], dlo_ref[2 * d + f], dhi_ref[2 * d + f])
            power = dl_s[0] + dl_s[1] * jnp.exp(LEAK_SLOPE * t_s[0, relc])
            rhs_s[relc] = inv_s[relc] * t_s[0, relc] + power

    def faces_z(l, c):
        gz_s[l] = harm(cond_s[l], cond_s[l + 1])
        return c

    lax.fori_loop(0, ze - 1, faces_z, 0)
    gz_s[ze - 1] = jnp.zeros((ye, xe), jnp.float32)

    def faces(l, c):
        cc = cond_s[l]
        gx = harm(cc, pltpu.roll(cc, xe - 1, 1))
        gx = jnp.where(lane == xe - 1, 0.0, gx)
        gy = harm(cc, pltpu.roll(cc, ye - 1, 0))
        gy = jnp.where(row == ye - 1, 0.0, gy)
        gxl = pltpu.roll(gx, 1, 1)
        gyu = pltpu.roll(gy, 1, 0)
        gx_s[l] = gx
        gxl_s[l] = gxl
        gy_s[l] = gy
        gyu_s[l] = gyu
        lm = jnp.maximum(l - 1, 0)
        gzm = jnp.where(l > 0, gz_s[lm], 0.0)
        sink = jnp.where(z0 + l == 0, SINK_CONDUCT, 0.0)
        diag = inv_s[l] + (gz_s[l] + gzm + gx + gxl + gy + gyu) + sink
        inv_s[l] = 1.0 / diag
        return c

    lax.fori_loop(0, ze, faces, 0)

    def relax(src, l):
        t = t_s[src, l]
        coupled = (gz_s[l] * t_s[src, l + 1] + gz_s[l - 1] * t_s[src, l - 1]
                   + gx_s[l] * pltpu.roll(t, xe - 1, 1) + gxl_s[l] * pltpu.roll(t, 1, 1)
                   + gy_s[l] * pltpu.roll(t, ye - 1, 0) + gyu_s[l] * pltpu.roll(t, 1, 0))
        return (rhs_s[l] + coupled) * inv_s[l]

    for k in range(1, SWEEPS):
        src, dst = (k - 1) % 2, k % 2

        def body(l, c, src=src, dst=dst):
            t_s[dst, l] = relax(src, l)
            return c

        lax.fori_loop(k, ze - k, body, 0)

    last = (SWEEPS - 1) % 2

    def final(i, c):
        new = relax(last, HALO + i)
        out_ref[i] = new[PAD_Y:PAD_Y + strip]
        return c

    lax.fori_loop(0, local_depth, final, 0)


def local(temp_old, material, conduct_table, capacity_table, dyn_power, leak_ref, die_layer):
    temp_start = temp_old[:, 0]
    cells_mat = material[:, 0]
    local_depth, nx, strip = temp_start.shape
    depth_n = lax.axis_size("depth")
    lat_n = lax.axis_size("lat")
    nz = local_depth * depth_n
    g = lax.axis_index("depth")
    s = lax.axis_index("lat")
    first_layer = g * local_depth
    layer_ids = first_layer + lax.iota(jnp.int32, local_depth)

    select = (die_layer[:, None] == layer_ids[None, :]).astype(jnp.float32)
    picked = jnp.einsum("dz,zxy->dxy", select, temp_start, precision=lax.Precision.HIGHEST)
    die_temp = lax.psum_scatter(picked, "depth", scatter_dimension=0, tiled=True)
    die_power = dyn_power[:, 0] + leak_ref[:, 0] * jnp.exp(LEAK_SLOPE * die_temp)

    tt = jnp.transpose(temp_start, (0, 2, 1))
    mt = jnp.transpose(cells_mat, (0, 2, 1)).astype(jnp.float32)
    tm = jnp.stack([tt, mt])
    dl = jnp.transpose(jnp.concatenate([dyn_power[:, 0], leak_ref[:, 0]]), (0, 2, 1))

    xb = from_behind(tm[:, local_depth - HALO:], "depth", 1)
    xa = from_behind(tm[:, :HALO], "depth", -1)
    rows = tm.reshape(2 * local_depth, strip, nx)
    ylo = from_behind(rows[:, strip - HALO:], "lat", 1)
    yhi = from_behind(rows[:, :HALO], "lat", -1)
    dc = lax.all_gather(dl, "depth", axis=0, tiled=False)

    ylo2 = ylo.reshape(2, local_depth, HALO, nx)
    yhi2 = yhi.reshape(2, local_depth, HALO, nx)
    side = jnp.concatenate([ylo2, yhi2], axis=2)
    cb = from_behind(side[:, local_depth - HALO:], "depth", 1)
    ca = from_behind(side[:, :HALO], "depth", -1)
    drows = dc.reshape(-1, strip, nx)
    dlo = from_behind(drows[:, strip - HALO:], "lat", 1)
    dhi = from_behind(drows[:, :HALO], "lat", -1)

    sc = jnp.concatenate([jnp.stack([g, s]).astype(jnp.int32), die_layer.astype(jnp.int32)])
    ze = local_depth + 2 * HALO
    ye = PAD_Y + strip + HALO + (-(PAD_Y + strip + HALO)) % 8
    smem = pl.BlockSpec(memory_space=pltpu.MemorySpace.SMEM)
    vmem = pl.BlockSpec(memory_space=pltpu.MemorySpace.VMEM)
    full = (ze, ye, nx)
    kern = functools.partial(sweep_kernel, nz, strip * lat_n, local_depth, strip)
    out = pl.pallas_call(
        kern,
        out_shape=jax.ShapeDtypeStruct((local_depth, strip, nx), jnp.float32),
        in_specs=[smem] * 3 + [vmem] * 10,
        out_specs=vmem,
        scratch_shapes=([pltpu.VMEM((2,) + full, jnp.float32)] + [pltpu.VMEM(full, jnp.float32)] * 8
                        + [pltpu.VMEM((2, ye, nx), jnp.float32)]),
        compiler_params=pltpu.CompilerParams(vmem_limit_bytes=60 * 1024 * 1024),
        interpret=INTERPRET,
    )(sc, conduct_table, capacity_table, tm, ylo, yhi, xb, xa, cb, ca, dc, dlo, dhi)
    temp_new = jnp.transpose(out, (0, 2, 1))
    return (temp_new[:, None], die_power[:, None])


def solution(mesh):
    return jax.shard_map(
        local,
        mesh=mesh,
        in_specs=(
            P("depth", "lat", None, None),
            P("depth", "lat", None, None),
            P(),
            P(),
            P("depth", "lat", None, None),
            P("depth", "lat", None, None),
            P(),
        ),
        out_specs=(P("depth", "lat", None, None), P("depth", "lat", None, None)),
        check_vma=False,
    )
```

```python
import functools

import jax
import jax.numpy as jnp
from jax import lax
from jax.experimental import pallas as pl
from jax.experimental.pallas import tpu as pltpu
from jax.sharding import PartitionSpec as P

SWEEPS = 6
HALO = SWEEPS
PAD_Y = 8

COND_SLOPE = 0.15
LEAK_SLOPE = 0.5
SINK_CONDUCT = 2.0

INTERPRET = False


def from_behind(block, axis, distance):
    devices = range(lax.axis_size(axis))
    route = [(i - distance, i) for i in devices if i - distance in devices]
    return lax.ppermute(block, axis, route)


def harm(a, b):
    summed = a + b
    return 2.0 * a * b / jnp.where(summed > 0, summed, 1.0)


def lookup(table_ref, material):
    looked = jnp.zeros(material.shape, jnp.float32)
    for entry in range(table_ref.shape[0]):
        looked = jnp.where(material == float(entry), table_ref[entry], looked)
    return looked


def sweep_kernel(nz, ny_total, local_depth, strip,
                 sc_ref, ctab_ref, htab_ref, xc_ref, xb_ref, xa_ref, dc_ref, ylo_ref, yhi_ref,
                 out_ref, t_s, cond_s, rhs_s, inv_s, gz_s, gx_s, gxl_s, gy_s, gyu_s, dl_s):
    ze = t_s.shape[1]
    ye = t_s.shape[2]
    xe = t_s.shape[3]
    g = sc_ref[0]
    s = sc_ref[1]
    z0 = g * local_depth - HALO
    row = lax.broadcasted_iota(jnp.int32, (ye, xe), 0)
    lane = lax.broadcasted_iota(jnp.int32, (ye, xe), 1)
    yg = s * strip + row - PAD_Y
    yvalid = (yg >= 0) & (yg < ny_total) & (row >= PAD_Y - HALO) & (row < PAD_Y + strip + HALO)
    top = PAD_Y + strip + HALO
    zlo = jnp.zeros((PAD_Y - HALO, xe), jnp.float32)
    zhi = jnp.zeros((ye - top, xe), jnp.float32)

    def put(dst, centre, lo, hi):
        dst[PAD_Y - HALO:PAD_Y] = lo
        dst[PAD_Y:PAD_Y + strip] = centre
        dst[PAD_Y + strip:top] = hi
        dst[0:PAD_Y - HALO] = zlo
        dst[top:ye] = zhi

    def tables(l, parts):
        for f, dst in ((0, t_s.at[0, l]), (1, cond_s.at[l])):
            put(dst, *parts[f])
        temp = t_s[0, l]
        mat = cond_s[l]
        zg = z0 + l
        valid = yvalid & (zg >= 0) & (zg < nz)
        cval = lookup(ctab_ref, mat)
        hval = lookup(htab_ref, mat)
        cond = jnp.where(valid, cval * jnp.exp(-COND_SLOPE * temp), 0.0)
        cond_s[l] = cond
        inv_s[l] = hval
        rhs_s[l] = hval * temp

    def below(i, c):
        tables(i, [(xb_ref[f, i], ylo_ref[2 * local_depth + f * HALO + i],
                    yhi_ref[2 * local_depth + f * HALO + i]) for f in range(2)])
        return c

    def centre(i, c):
        tables(HALO + i, [(xc_ref[f, i], ylo_ref[f * local_depth + i], yhi_ref[f * local_depth + i])
                          for f in range(2)])
        return c

    def above(i, c):
        tables(HALO + local_depth + i,
               [(xa_ref[f, i], ylo_ref[2 * local_depth + (2 + f) * HALO + i],
                 yhi_ref[2 * local_depth + (2 + f) * HALO + i]) for f in range(2)])
        return c

    lax.fori_loop(0, HALO, below, 0)
    lax.fori_loop(0, local_depth, centre, 0)
    lax.fori_loop(0, HALO, above, 0)

    dies = dc_ref.shape[0]
    dl_row = 2 * local_depth + 4 * HALO
    for o in range(dies):
        rel = sc_ref[2 + (g + dies - o) % dies] - z0
        relc = jnp.clip(rel, 0, ze - 1)

        @pl.when((rel >= 0) & (rel < ze))
        def _():
            for f in range(2):
                put(dl_s.at[f], dc_ref[o, f], ylo_ref[dl_row + 2 * o + f], yhi_ref[dl_row + 2 * o + f])
            power = dl_s[0] + dl_s[1] * jnp.exp(LEAK_SLOPE * t_s[0, relc])
            rhs_s[relc] = inv_s[relc] * t_s[0, relc] + power

    def faces_z(l, c):
        gz_s[l] = harm(cond_s[l], cond_s[l + 1])
        return c

    lax.fori_loop(0, ze - 1, faces_z, 0)
    gz_s[ze - 1] = jnp.zeros((ye, xe), jnp.float32)

    def faces(l, c):
        cc = cond_s[l]
        gx = harm(cc, pltpu.roll(cc, xe - 1, 1))
        gx = jnp.where(lane == xe - 1, 0.0, gx)
        gy = harm(cc, pltpu.roll(cc, ye - 1, 0))
        gy = jnp.where(row == ye - 1, 0.0, gy)
        gxl = pltpu.roll(gx, 1, 1)
        gyu = pltpu.roll(gy, 1, 0)
        gx_s[l] = gx
        gxl_s[l] = gxl
        gy_s[l] = gy
        gyu_s[l] = gyu
        lm = jnp.maximum(l - 1, 0)
        gzm = jnp.where(l > 0, gz_s[lm], 0.0)
        sink = jnp.where(z0 + l == 0, SINK_CONDUCT, 0.0)
        diag = inv_s[l] + (gz_s[l] + gzm + gx + gxl + gy + gyu) + sink
        inv_s[l] = 1.0 / diag
        return c

    lax.fori_loop(0, ze, faces, 0)

    def relax(src, l):
        t = t_s[src, l]
        coupled = (gz_s[l] * t_s[src, l + 1] + gz_s[l - 1] * t_s[src, l - 1]
                   + gx_s[l] * pltpu.roll(t, xe - 1, 1) + gxl_s[l] * pltpu.roll(t, 1, 1)
                   + gy_s[l] * pltpu.roll(t, ye - 1, 0) + gyu_s[l] * pltpu.roll(t, 1, 0))
        return (rhs_s[l] + coupled) * inv_s[l]

    for k in range(1, SWEEPS):
        src, dst = (k - 1) % 2, k % 2

        def body(l, c, src=src, dst=dst):
            t_s[dst, l] = relax(src, l)
            return c

        lax.fori_loop(k, ze - k, body, 0)

    last = (SWEEPS - 1) % 2

    def final(i, c):
        new = relax(last, HALO + i)
        out_ref[i] = new[PAD_Y:PAD_Y + strip]
        return c

    lax.fori_loop(0, local_depth, final, 0)


def local(temp_old, material, conduct_table, capacity_table, dyn_power, leak_ref, die_layer):
    temp_start = temp_old[:, 0]
    cells_mat = material[:, 0]
    local_depth, nx, strip = temp_start.shape
    depth_n = lax.axis_size("depth")
    lat_n = lax.axis_size("lat")
    dies = dyn_power.shape[0] * depth_n
    nz = local_depth * depth_n
    g = lax.axis_index("depth")
    s = lax.axis_index("lat")
    first_layer = g * local_depth

    tt = jnp.transpose(temp_start, (0, 2, 1))
    mt = jnp.transpose(cells_mat, (0, 2, 1)).astype(jnp.float32)
    tm = jnp.stack([tt, mt])
    dl = jnp.transpose(jnp.concatenate([dyn_power[:, 0], leak_ref[:, 0]]), (0, 2, 1))

    def pick(die):
        at = die_layer[die] - first_layer
        layer = lax.dynamic_index_in_dim(tt, jnp.clip(at, 0, local_depth - 1), 0, keepdims=True)
        return jnp.where((at >= 0) & (at < local_depth), layer, 0.0)

    xb = from_behind(tm[:, local_depth - HALO:], "depth", 1)
    xa = from_behind(tm[:, :HALO], "depth", -1)
    slots = [dl]
    die_temp = pick(g)
    for o in range(1, dies):
        route = [(i, (i + o) % depth_n) for i in range(depth_n)]
        sent = jnp.concatenate([dl, pick((g + o) % dies)])
        got = lax.ppermute(sent, "depth", route)
        slots.append(got[:2])
        die_temp = die_temp + got[2:]
    dc = jnp.stack(slots)
    die_temp = jnp.transpose(die_temp, (0, 2, 1))
    die_power = dyn_power[:, 0] + leak_ref[:, 0] * jnp.exp(LEAK_SLOPE * die_temp)

    held = [tm.reshape(-1, strip, nx), xb.reshape(-1, strip, nx), xa.reshape(-1, strip, nx),
            dc.reshape(-1, strip, nx)]
    ylo = from_behind(jnp.concatenate([h[:, strip - HALO:] for h in held]), "lat", 1)
    yhi = from_behind(jnp.concatenate([h[:, :HALO] for h in held]), "lat", -1)

    sc = jnp.concatenate([jnp.stack([g, s]).astype(jnp.int32), die_layer.astype(jnp.int32)])
    ze = local_depth + 2 * HALO
    ye = PAD_Y + strip + HALO + (-(PAD_Y + strip + HALO)) % 8
    smem = pl.BlockSpec(memory_space=pltpu.MemorySpace.SMEM)
    vmem = pl.BlockSpec(memory_space=pltpu.MemorySpace.VMEM)
    full = (ze, ye, nx)
    kern = functools.partial(sweep_kernel, nz, strip * lat_n, local_depth, strip)
    out = pl.pallas_call(
        kern,
        out_shape=jax.ShapeDtypeStruct((local_depth, strip, nx), jnp.float32),
        in_specs=[smem] * 3 + [vmem] * 6,
        out_specs=vmem,
        scratch_shapes=([pltpu.VMEM((2,) + full, jnp.float32)] + [pltpu.VMEM(full, jnp.float32)] * 8
                        + [pltpu.VMEM((2, ye, nx), jnp.float32)]),
        compiler_params=pltpu.CompilerParams(vmem_limit_bytes=60 * 1024 * 1024),
        interpret=INTERPRET,
    )(sc, conduct_table, capacity_table, tm, xb, xa, dc, ylo, yhi)
    temp_new = jnp.transpose(out, (0, 2, 1))
    return (temp_new[:, None], die_power[:, None])


def solution(mesh):
    return jax.shard_map(
        local,
        mesh=mesh,
        in_specs=(
            P("depth", "lat", None, None),
            P("depth", "lat", None, None),
            P(),
            P(),
            P("depth", "lat", None, None),
            P("depth", "lat", None, None),
            P(),
        ),
        out_specs=(P("depth", "lat", None, None), P("depth", "lat", None, None)),
        check_vma=False,
    )
```

```python
import functools

import jax
import jax.numpy as jnp
from jax import lax
from jax.experimental import pallas as pl
from jax.experimental.pallas import tpu as pltpu
from jax.sharding import PartitionSpec as P

SWEEPS = 6
HALO = SWEEPS
PAD_Y = 8

COND_SLOPE = 0.15
LEAK_SLOPE = 0.5
SINK_CONDUCT = 2.0

INTERPRET = False


def from_behind(block, axis, distance):
    devices = range(lax.axis_size(axis))
    route = [(i - distance, i) for i in devices if i - distance in devices]
    return lax.ppermute(block, axis, route)


def harm(a, b):
    summed = a + b
    return 2.0 * a * b / jnp.where(summed > 0, summed, 1.0)


def lookup(table_ref, material):
    looked = jnp.zeros(material.shape, jnp.float32)
    for entry in range(table_ref.shape[0]):
        looked = jnp.where(material == float(entry), table_ref[entry], looked)
    return looked


def sweep_kernel(nz, ny_total, local_depth, strip,
                 sc_ref, ctab_ref, htab_ref, tc_ref, mc_ref, tb_ref, mb_ref, ta_ref, ma_ref,
                 ylo_ref, yhi_ref, cb_ref, ca_ref, dc_ref,
                 out_ref, t_s, cond_s, rhs_s, inv_s, gz_s, gx_s, gxl_s, gy_s, gyu_s):
    ze = t_s.shape[1]
    ye = t_s.shape[2]
    xe = t_s.shape[3]
    g = sc_ref[0]
    s = sc_ref[1]
    z0 = g * local_depth - HALO
    row = lax.broadcasted_iota(jnp.int32, (ye, xe), 0)
    lane = lax.broadcasted_iota(jnp.int32, (ye, xe), 1)
    yg = s * strip + row - PAD_Y
    yvalid = (yg >= 0) & (yg < ny_total) & (row >= PAD_Y - HALO) & (row < PAD_Y + strip + HALO)
    top = PAD_Y + strip + HALO
    zlo = jnp.zeros((PAD_Y - HALO, xe), jnp.float32)
    zhi = jnp.zeros((ye - top, xe), jnp.float32)

    def put(dst, centre, lo, hi):
        dst[PAD_Y - HALO:PAD_Y] = lo
        dst[PAD_Y:PAD_Y + strip] = centre
        dst[PAD_Y + strip:top] = hi
        dst[0:PAD_Y - HALO] = zlo
        dst[top:ye] = zhi

    def tables(l, temp_raw, mat_raw, t_lo, t_hi, m_lo, m_hi):
        put(t_s.at[0, l], temp_raw.T, t_lo, t_hi)
        put(cond_s.at[l], mat_raw.T.astype(jnp.float32), m_lo, m_hi)
        temp = t_s[0, l]
        mat = cond_s[l]
        zg = z0 + l
        valid = yvalid & (zg >= 0) & (zg < nz)
        cval = lookup(ctab_ref, mat)
        hval = lookup(htab_ref, mat)
        cond = jnp.where(valid, cval * jnp.exp(-COND_SLOPE * temp), 0.0)
        cond_s[l] = cond
        inv_s[l] = hval
        rhs_s[l] = hval * temp

    def below(i, c):
        tables(i, tb_ref[i], mb_ref[i], cb_ref[0, i, :HALO], cb_ref[0, i, HALO:],
               cb_ref[1, i, :HALO], cb_ref[1, i, HALO:])
        return c

    def centre(i, c):
        tables(HALO + i, tc_ref[i], mc_ref[i], ylo_ref[i], yhi_ref[i],
               ylo_ref[local_depth + i], yhi_ref[local_depth + i])
        return c

    def above(i, c):
        tables(HALO + local_depth + i, ta_ref[i], ma_ref[i], ca_ref[0, i, :HALO], ca_ref[0, i, HALO:],
               ca_ref[1, i, :HALO], ca_ref[1, i, HALO:])
        return c

    lax.fori_loop(0, HALO, below, 0)
    lax.fori_loop(0, local_depth, centre, 0)
    lax.fori_loop(0, HALO, above, 0)

    dies = dc_ref.shape[0]
    for o in range(dies):
        rel = sc_ref[2 + (g + dies - o) % dies] - z0
        relc = jnp.clip(rel, 0, ze - 1)

        @pl.when((rel >= 0) & (rel < ze))
        def _():
            power = dc_ref[o, 0] + dc_ref[o, 1] * jnp.exp(LEAK_SLOPE * t_s[0, relc])
            rhs_s[relc] = inv_s[relc] * t_s[0, relc] + power

    def faces_z(l, c):
        gz_s[l] = harm(cond_s[l], cond_s[l + 1])
        return c

    lax.fori_loop(0, ze - 1, faces_z, 0)
    gz_s[ze - 1] = jnp.zeros((ye, xe), jnp.float32)

    def faces(l, c):
        cc = cond_s[l]
        gx = harm(cc, pltpu.roll(cc, xe - 1, 1))
        gx = jnp.where(lane == xe - 1, 0.0, gx)
        gy = harm(cc, pltpu.roll(cc, ye - 1, 0))
        gy = jnp.where(row == ye - 1, 0.0, gy)
        gxl = pltpu.roll(gx, 1, 1)
        gyu = pltpu.roll(gy, 1, 0)
        gx_s[l] = gx
        gxl_s[l] = gxl
        gy_s[l] = gy
        gyu_s[l] = gyu
        lm = jnp.maximum(l - 1, 0)
        gzm = jnp.where(l > 0, gz_s[lm], 0.0)
        sink = jnp.where(z0 + l == 0, SINK_CONDUCT, 0.0)
        diag = inv_s[l] + (gz_s[l] + gzm + gx + gxl + gy + gyu) + sink
        inv_s[l] = 1.0 / diag
        return c

    lax.fori_loop(0, ze, faces, 0)

    def relax(src, l):
        t = t_s[src, l]
        coupled = (gz_s[l] * t_s[src, l + 1] + gz_s[l - 1] * t_s[src, l - 1]
                   + gx_s[l] * pltpu.roll(t, xe - 1, 1) + gxl_s[l] * pltpu.roll(t, 1, 1)
                   + gy_s[l] * pltpu.roll(t, ye - 1, 0) + gyu_s[l] * pltpu.roll(t, 1, 0))
        return (rhs_s[l] + coupled) * inv_s[l]

    for k in range(1, SWEEPS):
        src, dst = (k - 1) % 2, k % 2

        def body(l, c, src=src, dst=dst):
            t_s[dst, l] = relax(src, l)
            return c

        lax.fori_loop(k, ze - k, body, 0)

    last = (SWEEPS - 1) % 2

    def final(i, c):
        new = relax(last, HALO + i)
        out_ref[i] = new[PAD_Y:PAD_Y + strip].T
        return c

    lax.fori_loop(0, local_depth, final, 0)


def local(temp_old, material, conduct_table, capacity_table, dyn_power, leak_ref, die_layer):
    temp_start = temp_old[:, 0]
    cells_mat = material[:, 0]
    local_depth, nx, strip = temp_start.shape
    depth_n = lax.axis_size("depth")
    lat_n = lax.axis_size("lat")
    dies = dyn_power.shape[0] * depth_n
    nz = local_depth * depth_n
    g = lax.axis_index("depth")
    s = lax.axis_index("lat")
    first_layer = g * local_depth

    def pick(die):
        at = die_layer[die] - first_layer
        layer = lax.dynamic_index_in_dim(temp_start, jnp.clip(at, 0, local_depth - 1), 0, keepdims=True)
        return jnp.where((at >= 0) & (at < local_depth), layer, 0.0)

    tb = from_behind(temp_start[local_depth - HALO:], "depth", 1)
    mb = from_behind(cells_mat[local_depth - HALO:], "depth", 1)
    ta = from_behind(temp_start[:HALO], "depth", -1)
    ma = from_behind(cells_mat[:HALO], "depth", -1)
    die_temp = pick(g)
    for o in range(1, dies):
        route = [(i, (i + o) % depth_n) for i in range(depth_n)]
        die_temp = die_temp + lax.ppermute(pick((g + o) % dies), "depth", route)
    die_power = dyn_power[:, 0] + leak_ref[:, 0] * jnp.exp(LEAK_SLOPE * die_temp)

    fields = jnp.concatenate([temp_start, cells_mat.astype(jnp.float32), dyn_power[:, 0], leak_ref[:, 0]])
    nf = fields.shape[0]
    last_cols = jnp.transpose(fields[:, :, strip - HALO:], (0, 2, 1))
    first_cols = jnp.transpose(fields[:, :, :HALO], (0, 2, 1))
    ylo = from_behind(last_cols, "lat", 1)
    yhi = from_behind(first_cols, "lat", -1)

    ye = PAD_Y + strip + HALO + (-(PAD_Y + strip + HALO)) % 8
    side = jnp.concatenate([ylo[:2 * local_depth].reshape(2, local_depth, HALO, nx),
                            yhi[:2 * local_depth].reshape(2, local_depth, HALO, nx)], axis=2)
    cb = from_behind(side[:, local_depth - HALO:], "depth", 1)
    ca = from_behind(side[:, :HALO], "depth", -1)
    dl = jnp.concatenate([
        jnp.zeros((2, PAD_Y - HALO, nx), jnp.float32), ylo[nf - 2:],
        jnp.transpose(jnp.concatenate([dyn_power[:, 0], leak_ref[:, 0]]), (0, 2, 1)),
        yhi[nf - 2:], jnp.zeros((2, ye - (PAD_Y + strip + HALO), nx), jnp.float32)], axis=1)
    slots = [dl]
    for o in range(1, dies):
        route = [(i, (i + o) % depth_n) for i in range(depth_n)]
        slots.append(lax.ppermute(dl, "depth", route))
    dc = jnp.stack(slots)

    sc = jnp.concatenate([jnp.stack([g, s]).astype(jnp.int32), die_layer.astype(jnp.int32)])
    ze = local_depth + 2 * HALO
    smem = pl.BlockSpec(memory_space=pltpu.MemorySpace.SMEM)
    vmem = pl.BlockSpec(memory_space=pltpu.MemorySpace.VMEM)
    full = (ze, ye, nx)
    kern = functools.partial(sweep_kernel, nz, strip * lat_n, local_depth, strip)
    out = pl.pallas_call(
        kern,
        out_shape=jax.ShapeDtypeStruct((local_depth, nx, strip), jnp.float32),
        in_specs=[smem] * 3 + [vmem] * 11,
        out_specs=vmem,
        scratch_shapes=([pltpu.VMEM((2,) + full, jnp.float32)] + [pltpu.VMEM(full, jnp.float32)] * 8),
        compiler_params=pltpu.CompilerParams(vmem_limit_bytes=60 * 1024 * 1024),
        interpret=INTERPRET,
    )(sc, conduct_table, capacity_table, temp_start, cells_mat, tb, mb, ta, ma, ylo, yhi, cb, ca, dc)
    return (out[:, None], die_power[:, None])


def solution(mesh):
    return jax.shard_map(
        local,
        mesh=mesh,
        in_specs=(
            P("depth", "lat", None, None),
            P("depth", "lat", None, None),
            P(),
            P(),
            P("depth", "lat", None, None),
            P("depth", "lat", None, None),
            P(),
        ),
        out_specs=(P("depth", "lat", None, None), P("depth", "lat", None, None)),
        check_vma=False,
    )
```

```python
import functools

import jax
import jax.numpy as jnp
from jax import lax
from jax.experimental import pallas as pl
from jax.experimental.pallas import tpu as pltpu
from jax.sharding import PartitionSpec as P

SWEEPS = 6
HALO = SWEEPS
PAD_Y = 8

COND_SLOPE = 0.15
LEAK_SLOPE = 0.5
SINK_CONDUCT = 2.0

INTERPRET = False


def from_behind(block, axis, distance):
    devices = range(lax.axis_size(axis))
    route = [(i - distance, i) for i in devices if i - distance in devices]
    return lax.ppermute(block, axis, route)


def harm(a, b):
    summed = a + b
    return 2.0 * a * b / jnp.where(summed > 0, summed, 1.0)


def lookup(table_ref, material):
    looked = jnp.zeros(material.shape, jnp.float32)
    for entry in range(table_ref.shape[0]):
        looked = jnp.where(material == float(entry), table_ref[entry], looked)
    return looked


def sweep_kernel(nz, ny_total, local_depth, strip,
                 sc_ref, ctab_ref, htab_ref, tc_ref, mc_ref, xb_ref, xa_ref,
                 ylo_ref, yhi_ref, cb_ref, ca_ref, d0_ref, d1_ref, d2_ref, d3_ref,
                 out_ref, t_s, cond_s, rhs_s, inv_s, gz_s, gx_s, gxl_s, gy_s, gyu_s):
    ze = t_s.shape[1]
    ye = t_s.shape[2]
    xe = t_s.shape[3]
    g = sc_ref[0]
    s = sc_ref[1]
    z0 = g * local_depth - HALO
    row = lax.broadcasted_iota(jnp.int32, (ye, xe), 0)
    lane = lax.broadcasted_iota(jnp.int32, (ye, xe), 1)
    yg = s * strip + row - PAD_Y
    yvalid = (yg >= 0) & (yg < ny_total) & (row >= PAD_Y - HALO) & (row < PAD_Y + strip + HALO)
    top = PAD_Y + strip + HALO
    zlo = jnp.zeros((PAD_Y - HALO, xe), jnp.float32)
    zhi = jnp.zeros((ye - top, xe), jnp.float32)

    def put(dst, centre, lo, hi):
        dst[PAD_Y - HALO:PAD_Y] = lo
        dst[PAD_Y:PAD_Y + strip] = centre
        dst[PAD_Y + strip:top] = hi
        dst[0:PAD_Y - HALO] = zlo
        dst[top:ye] = zhi

    def tables(l, temp_raw, mat_raw, t_lo, t_hi, m_lo, m_hi):
        put(t_s.at[0, l], temp_raw.T, t_lo, t_hi)
        put(cond_s.at[l], mat_raw.T.astype(jnp.float32), m_lo, m_hi)
        temp = t_s[0, l]
        mat = cond_s[l]
        zg = z0 + l
        valid = yvalid & (zg >= 0) & (zg < nz)
        cval = lookup(ctab_ref, mat)
        hval = lookup(htab_ref, mat)
        cond = jnp.where(valid, cval * jnp.exp(-COND_SLOPE * temp), 0.0)
        cond_s[l] = cond
        inv_s[l] = hval
        rhs_s[l] = hval * temp

    def below(i, c):
        tables(i, xb_ref[0, i], xb_ref[1, i], cb_ref[0, i, :HALO], cb_ref[0, i, HALO:],
               cb_ref[1, i, :HALO], cb_ref[1, i, HALO:])
        return c

    def centre(i, c):
        tables(HALO + i, tc_ref[i], mc_ref[i], ylo_ref[i], yhi_ref[i],
               ylo_ref[local_depth + i], yhi_ref[local_depth + i])
        return c

    def above(i, c):
        tables(HALO + local_depth + i, xa_ref[0, i], xa_ref[1, i], ca_ref[0, i, :HALO], ca_ref[0, i, HALO:],
               ca_ref[1, i, :HALO], ca_ref[1, i, HALO:])
        return c

    lax.fori_loop(0, HALO, below, 0)
    lax.fori_loop(0, local_depth, centre, 0)
    lax.fori_loop(0, HALO, above, 0)

    slots = (d0_ref, d1_ref, d2_ref, d3_ref)
    dies = len(slots)
    for o in range(dies):
        rel = sc_ref[2 + (g + dies - o) % dies] - z0
        relc = jnp.clip(rel, 0, ze - 1)

        @pl.when((rel >= 0) & (rel < ze))
        def _():
            power = slots[o][0] + slots[o][1] * jnp.exp(LEAK_SLOPE * t_s[0, relc])
            rhs_s[relc] = inv_s[relc] * t_s[0, relc] + power

    def faces_z(l, c):
        gz_s[l] = harm(cond_s[l], cond_s[l + 1])
        return c

    lax.fori_loop(0, ze - 1, faces_z, 0)
    gz_s[ze - 1] = jnp.zeros((ye, xe), jnp.float32)

    def faces(l, c):
        cc = cond_s[l]
        gx = harm(cc, pltpu.roll(cc, xe - 1, 1))
        gx = jnp.where(lane == xe - 1, 0.0, gx)
        gy = harm(cc, pltpu.roll(cc, ye - 1, 0))
        gy = jnp.where(row == ye - 1, 0.0, gy)
        gxl = pltpu.roll(gx, 1, 1)
        gyu = pltpu.roll(gy, 1, 0)
        gx_s[l] = gx
        gxl_s[l] = gxl
        gy_s[l] = gy
        gyu_s[l] = gyu
        lm = jnp.maximum(l - 1, 0)
        gzm = jnp.where(l > 0, gz_s[lm], 0.0)
        sink = jnp.where(z0 + l == 0, SINK_CONDUCT, 0.0)
        diag = inv_s[l] + (gz_s[l] + gzm + gx + gxl + gy + gyu) + sink
        inv_s[l] = 1.0 / diag
        return c

    lax.fori_loop(0, ze, faces, 0)

    def relax(src, l):
        t = t_s[src, l]
        coupled = (gz_s[l] * t_s[src, l + 1] + gz_s[l - 1] * t_s[src, l - 1]
                   + gx_s[l] * pltpu.roll(t, xe - 1, 1) + gxl_s[l] * pltpu.roll(t, 1, 1)
                   + gy_s[l] * pltpu.roll(t, ye - 1, 0) + gyu_s[l] * pltpu.roll(t, 1, 0))
        return (rhs_s[l] + coupled) * inv_s[l]

    for k in range(1, SWEEPS):
        src, dst = (k - 1) % 2, k % 2

        def body(l, c, src=src, dst=dst):
            t_s[dst, l] = relax(src, l)
            return c

        lax.fori_loop(k, ze - k, body, 0)

    last = (SWEEPS - 1) % 2

    def final(i, c):
        new = relax(last, HALO + i)
        out_ref[i] = new[PAD_Y:PAD_Y + strip].T
        return c

    lax.fori_loop(0, local_depth, final, 0)


def local(temp_old, material, conduct_table, capacity_table, dyn_power, leak_ref, die_layer):
    temp_start = temp_old[:, 0]
    cells_mat = material[:, 0]
    local_depth, nx, strip = temp_start.shape
    depth_n = lax.axis_size("depth")
    lat_n = lax.axis_size("lat")
    dies = dyn_power.shape[0] * depth_n
    nz = local_depth * depth_n
    g = lax.axis_index("depth")
    s = lax.axis_index("lat")
    first_layer = g * local_depth
    ye = PAD_Y + strip + HALO + (-(PAD_Y + strip + HALO)) % 8

    stacked = jnp.stack([temp_start, cells_mat.astype(jnp.float32)])
    xb = from_behind(stacked[:, local_depth - HALO:], "depth", 1)
    xa = from_behind(stacked[:, :HALO], "depth", -1)
    fields = jnp.concatenate([stacked.reshape(-1, nx, strip), dyn_power[:, 0], leak_ref[:, 0]])
    nf = fields.shape[0]
    ylo = from_behind(jnp.transpose(fields[:, :, strip - HALO:], (0, 2, 1)), "lat", 1)
    yhi = from_behind(jnp.transpose(fields[:, :, :HALO], (0, 2, 1)), "lat", -1)

    dl = jnp.concatenate([
        jnp.zeros((2, PAD_Y - HALO, nx), jnp.float32), ylo[nf - 2:],
        jnp.transpose(jnp.concatenate([dyn_power[:, 0], leak_ref[:, 0]]), (0, 2, 1)),
        yhi[nf - 2:], jnp.zeros((2, ye - (PAD_Y + strip + HALO), nx), jnp.float32)], axis=1)
    side = jnp.concatenate([ylo[:2 * local_depth].reshape(2, local_depth, HALO, nx),
                            yhi[:2 * local_depth].reshape(2, local_depth, HALO, nx)], axis=2)

    def pick(die):
        at = die_layer[die] - first_layer
        layer = lax.dynamic_index_in_dim(temp_start, jnp.clip(at, 0, local_depth - 1), 0, keepdims=False)
        layer = jnp.where((at >= 0) & (at < local_depth), layer, 0.0).T
        return jnp.pad(layer, ((0, ye - strip), (0, 0)))[None]

    corner_rows = 2 * HALO * 2 * HALO
    die_temp = pick(g)[0, :strip]
    slots = [dl]
    cb = ca = None
    for o in range(1, dies):
        route = [(i, (i + o) % depth_n) for i in range(depth_n)]
        parts = [dl.reshape(-1, nx), pick((g + o) % dies).reshape(-1, nx)]
        if o == 1:
            parts.append(side[:, local_depth - HALO:].reshape(-1, nx))
        if o == dies - 1:
            parts.append(side[:, :HALO].reshape(-1, nx))
        got = lax.ppermute(jnp.concatenate(parts), "depth", route)
        slots.append(got[:2 * ye].reshape(2, ye, nx))
        die_temp = die_temp + got[2 * ye:2 * ye + strip]
        if o == 1:
            cb = got[3 * ye:3 * ye + corner_rows].reshape(2, HALO, 2 * HALO, nx)
        if o == dies - 1:
            ca = got[3 * ye:3 * ye + corner_rows].reshape(2, HALO, 2 * HALO, nx)
    die_temp = die_temp.T[None]
    die_power = dyn_power[:, 0] + leak_ref[:, 0] * jnp.exp(LEAK_SLOPE * die_temp)

    sc = jnp.concatenate([jnp.stack([g, s]).astype(jnp.int32), die_layer.astype(jnp.int32)])
    ze = local_depth + 2 * HALO
    smem = pl.BlockSpec(memory_space=pltpu.MemorySpace.SMEM)
    vmem = pl.BlockSpec(memory_space=pltpu.MemorySpace.VMEM)
    full = (ze, ye, nx)
    kern = functools.partial(sweep_kernel, nz, strip * lat_n, local_depth, strip)
    out = pl.pallas_call(
        kern,
        out_shape=jax.ShapeDtypeStruct((local_depth, nx, strip), jnp.float32),
        in_specs=[smem] * 3 + [vmem] * 12,
        out_specs=vmem,
        scratch_shapes=([pltpu.VMEM((2,) + full, jnp.float32)] + [pltpu.VMEM(full, jnp.float32)] * 8),
        compiler_params=pltpu.CompilerParams(vmem_limit_bytes=60 * 1024 * 1024),
        interpret=INTERPRET,
    )(sc, conduct_table, capacity_table, temp_start, cells_mat, xb, xa, ylo, yhi, cb, ca, *slots)
    return (out[:, None], die_power[:, None])


def solution(mesh):
    return jax.shard_map(
        local,
        mesh=mesh,
        in_specs=(
            P("depth", "lat", None, None),
            P("depth", "lat", None, None),
            P(),
            P(),
            P("depth", "lat", None, None),
            P("depth", "lat", None, None),
            P(),
        ),
        out_specs=(P("depth", "lat", None, None), P("depth", "lat", None, None)),
        check_vma=False,
    )
```

```python
import functools

import jax
import jax.numpy as jnp
from jax import lax
from jax.experimental import pallas as pl
from jax.experimental.pallas import tpu as pltpu
from jax.sharding import PartitionSpec as P

SWEEPS = 6
HALO = SWEEPS
PAD_Y = 8

COND_SLOPE = 0.15
LEAK_SLOPE = 0.5
SINK_CONDUCT = 2.0

INTERPRET = False


def from_behind(block, axis, distance):
    devices = range(lax.axis_size(axis))
    route = [(i - distance, i) for i in devices if i - distance in devices]
    return lax.ppermute(block, axis, route)


def harm(a, b):
    summed = a + b
    return 2.0 * a * b / jnp.where(summed > 0, summed, 1.0)


def lookup(table_ref, material):
    looked = jnp.zeros(material.shape, jnp.float32)
    for entry in range(table_ref.shape[0]):
        looked = jnp.where(material == float(entry), table_ref[entry], looked)
    return looked


def sweep_kernel(nz, ny_total, local_depth, strip,
                 sc_ref, ctab_ref, htab_ref, tc_ref, mc_ref, xb_ref, xa_ref,
                 ylo_ref, yhi_ref, cb_ref, ca_ref, d0_ref, d1_ref, d2_ref, d3_ref,
                 out_ref, t_s, cond_s, rhs_s, inv_s, gz_s, gx_s, gxl_s, gy_s, gyu_s):
    ze = t_s.shape[1]
    ye = t_s.shape[2]
    xe = t_s.shape[3]
    g = sc_ref[0]
    s = sc_ref[1]
    z0 = g * local_depth - HALO
    row = lax.broadcasted_iota(jnp.int32, (ye, xe), 0)
    lane = lax.broadcasted_iota(jnp.int32, (ye, xe), 1)
    yg = s * strip + row - PAD_Y
    yvalid = (yg >= 0) & (yg < ny_total) & (row >= PAD_Y - HALO) & (row < PAD_Y + strip + HALO)
    top = PAD_Y + strip + HALO
    zlo = jnp.zeros((PAD_Y - HALO, xe), jnp.float32)
    zhi = jnp.zeros((ye - top, xe), jnp.float32)

    def put(dst, centre, lo, hi):
        dst[PAD_Y - HALO:PAD_Y] = lo
        dst[PAD_Y:PAD_Y + strip] = centre
        dst[PAD_Y + strip:top] = hi
        dst[0:PAD_Y - HALO] = zlo
        dst[top:ye] = zhi

    def tables(l, temp_raw, mat_raw, t_lo, t_hi, m_lo, m_hi):
        put(t_s.at[0, l], temp_raw.T, t_lo, t_hi)
        put(cond_s.at[l], mat_raw.T.astype(jnp.float32), m_lo, m_hi)
        temp = t_s[0, l]
        mat = cond_s[l]
        zg = z0 + l
        valid = yvalid & (zg >= 0) & (zg < nz)
        cval = lookup(ctab_ref, mat)
        hval = lookup(htab_ref, mat)
        cond = jnp.where(valid, cval * jnp.exp(-COND_SLOPE * temp), 0.0)
        cond_s[l] = cond
        inv_s[l] = hval
        rhs_s[l] = hval * temp

    def below(i, c):
        tables(i, xb_ref[0, i], xb_ref[1, i], cb_ref[0, i, :HALO], cb_ref[0, i, HALO:],
               cb_ref[1, i, :HALO], cb_ref[1, i, HALO:])
        return c

    def centre(i, c):
        tables(HALO + i, tc_ref[i], mc_ref[i], ylo_ref[i], yhi_ref[i],
               ylo_ref[local_depth + i], yhi_ref[local_depth + i])
        return c

    def above(i, c):
        tables(HALO + local_depth + i, xa_ref[0, i], xa_ref[1, i], ca_ref[0, i, :HALO], ca_ref[0, i, HALO:],
               ca_ref[1, i, :HALO], ca_ref[1, i, HALO:])
        return c

    lax.fori_loop(0, HALO, below, 0)
    lax.fori_loop(0, local_depth, centre, 0)
    lax.fori_loop(0, HALO, above, 0)

    slots = (d0_ref, d1_ref, d2_ref, d3_ref)
    dies = len(slots)
    for o in range(dies):
        rel = sc_ref[2 + (g + dies - o) % dies] - z0
        relc = jnp.clip(rel, 0, ze - 1)

        @pl.when((rel >= 0) & (rel < ze))
        def _():
            rhs_s[relc] = inv_s[relc] * t_s[0, relc] + slots[o][...]

    def faces_z(l, c):
        gz_s[l] = harm(cond_s[l], cond_s[l + 1])
        return c

    lax.fori_loop(0, ze - 1, faces_z, 0)
    gz_s[ze - 1] = jnp.zeros((ye, xe), jnp.float32)

    def faces(l, c):
        cc = cond_s[l]
        gx = harm(cc, pltpu.roll(cc, xe - 1, 1))
        gx = jnp.where(lane == xe - 1, 0.0, gx)
        gy = harm(cc, pltpu.roll(cc, ye - 1, 0))
        gy = jnp.where(row == ye - 1, 0.0, gy)
        gxl = pltpu.roll(gx, 1, 1)
        gyu = pltpu.roll(gy, 1, 0)
        gx_s[l] = gx
        gxl_s[l] = gxl
        gy_s[l] = gy
        gyu_s[l] = gyu
        lm = jnp.maximum(l - 1, 0)
        gzm = jnp.where(l > 0, gz_s[lm], 0.0)
        sink = jnp.where(z0 + l == 0, SINK_CONDUCT, 0.0)
        diag = inv_s[l] + (gz_s[l] + gzm + gx + gxl + gy + gyu) + sink
        inv_s[l] = 1.0 / diag
        return c

    lax.fori_loop(0, ze, faces, 0)

    def relax(src, l):
        t = t_s[src, l]
        coupled = (gz_s[l] * t_s[src, l + 1] + gz_s[l - 1] * t_s[src, l - 1]
                   + gx_s[l] * pltpu.roll(t, xe - 1, 1) + gxl_s[l] * pltpu.roll(t, 1, 1)
                   + gy_s[l] * pltpu.roll(t, ye - 1, 0) + gyu_s[l] * pltpu.roll(t, 1, 0))
        return (rhs_s[l] + coupled) * inv_s[l]

    for k in range(1, SWEEPS):
        src, dst = (k - 1) % 2, k % 2

        def body(l, c, src=src, dst=dst):
            t_s[dst, l] = relax(src, l)
            return c

        lax.fori_loop(k, ze - k, body, 0)

    last = (SWEEPS - 1) % 2

    def final(i, c):
        new = relax(last, HALO + i)
        out_ref[i] = new[PAD_Y:PAD_Y + strip].T
        return c

    lax.fori_loop(0, local_depth, final, 0)


def local(temp_old, material, conduct_table, capacity_table, dyn_power, leak_ref, die_layer):
    temp_start = temp_old[:, 0]
    cells_mat = material[:, 0]
    local_depth, nx, strip = temp_start.shape
    depth_n = lax.axis_size("depth")
    lat_n = lax.axis_size("lat")
    dies = dyn_power.shape[0] * depth_n
    nz = local_depth * depth_n
    g = lax.axis_index("depth")
    s = lax.axis_index("lat")
    first_layer = g * local_depth
    ye = PAD_Y + strip + HALO + (-(PAD_Y + strip + HALO)) % 8

    stacked = jnp.stack([temp_start, cells_mat.astype(jnp.float32)])
    xb = from_behind(stacked[:, local_depth - HALO:], "depth", 1)
    xa = from_behind(stacked[:, :HALO], "depth", -1)
    fields = jnp.concatenate([stacked.reshape(-1, nx, strip), dyn_power[:, 0], leak_ref[:, 0]])
    nf = fields.shape[0]
    ylo = from_behind(jnp.transpose(fields[:, :, strip - HALO:], (0, 2, 1)), "lat", 1)
    yhi = from_behind(jnp.transpose(fields[:, :, :HALO], (0, 2, 1)), "lat", -1)

    def widen(centre, lo, hi):
        return jnp.concatenate([jnp.zeros((PAD_Y - HALO, nx), jnp.float32), lo, centre, hi,
                                jnp.zeros((ye - (PAD_Y + strip + HALO), nx), jnp.float32)])

    side = jnp.concatenate([ylo[:2 * local_depth].reshape(2, local_depth, HALO, nx),
                            yhi[:2 * local_depth].reshape(2, local_depth, HALO, nx)], axis=2)
    cb = from_behind(side[:, local_depth - HALO:], "depth", 1)
    ca = from_behind(side[:, :HALO], "depth", -1)

    def pick(die):
        at = die_layer[die] - first_layer
        atc = jnp.clip(at, 0, local_depth - 1)
        layer = widen(lax.dynamic_index_in_dim(temp_start, atc, 0, keepdims=False).T,
                      lax.dynamic_index_in_dim(ylo, atc, 0, keepdims=False),
                      lax.dynamic_index_in_dim(yhi, atc, 0, keepdims=False))
        return jnp.where((at >= 0) & (at < local_depth), layer, 0.0)

    die_temp = pick(g)
    for o in range(1, dies):
        route = [(i, (i + o) % depth_n) for i in range(depth_n)]
        die_temp = die_temp + lax.ppermute(pick((g + o) % dies), "depth", route)
    dyn_w = widen(dyn_power[0, 0].T, ylo[nf - 2], yhi[nf - 2])
    leak_w = widen(leak_ref[0, 0].T, ylo[nf - 1], yhi[nf - 1])
    power_w = dyn_w + leak_w * jnp.exp(LEAK_SLOPE * die_temp)
    die_power = power_w[PAD_Y:PAD_Y + strip].T[None]

    slots = [power_w]
    for o in range(1, dies):
        route = [(i, (i + o) % depth_n) for i in range(depth_n)]
        slots.append(lax.ppermute(power_w, "depth", route))

    sc = jnp.concatenate([jnp.stack([g, s]).astype(jnp.int32), die_layer.astype(jnp.int32)])
    ze = local_depth + 2 * HALO
    smem = pl.BlockSpec(memory_space=pltpu.MemorySpace.SMEM)
    vmem = pl.BlockSpec(memory_space=pltpu.MemorySpace.VMEM)
    full = (ze, ye, nx)
    kern = functools.partial(sweep_kernel, nz, strip * lat_n, local_depth, strip)
    out = pl.pallas_call(
        kern,
        out_shape=jax.ShapeDtypeStruct((local_depth, nx, strip), jnp.float32),
        in_specs=[smem] * 3 + [vmem] * 12,
        out_specs=vmem,
        scratch_shapes=([pltpu.VMEM((2,) + full, jnp.float32)] + [pltpu.VMEM(full, jnp.float32)] * 8),
        compiler_params=pltpu.CompilerParams(vmem_limit_bytes=60 * 1024 * 1024),
        interpret=INTERPRET,
    )(sc, conduct_table, capacity_table, temp_start, cells_mat, xb, xa, ylo, yhi, cb, ca, *slots)
    return (out[:, None], die_power[:, None])


def solution(mesh):
    return jax.shard_map(
        local,
        mesh=mesh,
        in_specs=(
            P("depth", "lat", None, None),
            P("depth", "lat", None, None),
            P(),
            P(),
            P("depth", "lat", None, None),
            P("depth", "lat", None, None),
            P(),
        ),
        out_specs=(P("depth", "lat", None, None), P("depth", "lat", None, None)),
        check_vma=False,
    )
```

```python
import functools

import jax
import jax.numpy as jnp
from jax import lax
from jax.experimental import pallas as pl
from jax.experimental.pallas import tpu as pltpu
from jax.sharding import PartitionSpec as P

SWEEPS = 6
HALO = SWEEPS
PAD_Y = 8

COND_SLOPE = 0.15
LEAK_SLOPE = 0.5
SINK_CONDUCT = 2.0

INTERPRET = False


def from_behind(block, axis, distance):
    devices = range(lax.axis_size(axis))
    route = [(i - distance, i) for i in devices if i - distance in devices]
    return lax.ppermute(block, axis, route)


def harm(a, b):
    summed = a + b
    return 2.0 * a * b / jnp.where(summed > 0, summed, 1.0)


def lookup(table_ref, material):
    looked = jnp.zeros(material.shape, jnp.float32)
    for entry in range(table_ref.shape[0]):
        looked = jnp.where(material == float(entry), table_ref[entry], looked)
    return looked


def sweep_kernel(nz, ny_total, local_depth, strip,
                 sc_ref, ctab_ref, htab_ref, tc_ref, mc_ref, tb_ref, mb_ref, ta_ref, ma_ref,
                 ylo_ref, yhi_ref, cb_ref, ca_ref, d0_ref, d1_ref, d2_ref, d3_ref,
                 out_ref, t_s, cond_s, rhs_s, inv_s, gz_s, gx_s, gxl_s, gy_s, gyu_s):
    ze = t_s.shape[1]
    ye = t_s.shape[2]
    xe = t_s.shape[3]
    g = sc_ref[0]
    s = sc_ref[1]
    z0 = g * local_depth - HALO
    row = lax.broadcasted_iota(jnp.int32, (ye, xe), 0)
    lane = lax.broadcasted_iota(jnp.int32, (ye, xe), 1)
    yg = s * strip + row - PAD_Y
    yvalid = (yg >= 0) & (yg < ny_total) & (row >= PAD_Y - HALO) & (row < PAD_Y + strip + HALO)
    top = PAD_Y + strip + HALO
    zlo = jnp.zeros((PAD_Y - HALO, xe), jnp.float32)
    zhi = jnp.zeros((ye - top, xe), jnp.float32)

    def put(dst, centre, lo, hi):
        dst[PAD_Y - HALO:PAD_Y] = lo
        dst[PAD_Y:PAD_Y + strip] = centre
        dst[PAD_Y + strip:top] = hi
        dst[0:PAD_Y - HALO] = zlo
        dst[top:ye] = zhi

    def tables(l, temp_raw, mat_raw, t_lo, t_hi, m_lo, m_hi):
        put(t_s.at[0, l], temp_raw.T, t_lo, t_hi)
        put(cond_s.at[l], mat_raw.T.astype(jnp.float32), m_lo, m_hi)
        temp = t_s[0, l]
        mat = cond_s[l]
        zg = z0 + l
        valid = yvalid & (zg >= 0) & (zg < nz)
        cval = lookup(ctab_ref, mat)
        hval = lookup(htab_ref, mat)
        cond = jnp.where(valid, cval * jnp.exp(-COND_SLOPE * temp), 0.0)
        cond_s[l] = cond
        inv_s[l] = hval
        rhs_s[l] = hval * temp

    def below(i, c):
        tables(i, tb_ref[i], mb_ref[i], cb_ref[0, i, :HALO], cb_ref[0, i, HALO:],
               cb_ref[1, i, :HALO], cb_ref[1, i, HALO:])
        return c

    def centre(i, c):
        tables(HALO + i, tc_ref[i], mc_ref[i], ylo_ref[i], yhi_ref[i],
               ylo_ref[local_depth + i], yhi_ref[local_depth + i])
        return c

    def above(i, c):
        tables(HALO + local_depth + i, ta_ref[i], ma_ref[i], ca_ref[0, i, :HALO], ca_ref[0, i, HALO:],
               ca_ref[1, i, :HALO], ca_ref[1, i, HALO:])
        return c

    lax.fori_loop(0, HALO, below, 0)
    lax.fori_loop(0, local_depth, centre, 0)
    lax.fori_loop(0, HALO, above, 0)

    slots = (d0_ref, d1_ref, d2_ref, d3_ref)
    dies = len(slots)
    for o in range(dies):
        rel = sc_ref[2 + (g + dies - o) % dies] - z0
        relc = jnp.clip(rel, 0, ze - 1)

        @pl.when((rel >= 0) & (rel < ze))
        def _():
            rhs_s[relc] = inv_s[relc] * t_s[0, relc] + slots[o][...]

    def faces_z(l, c):
        gz_s[l] = harm(cond_s[l], cond_s[l + 1])
        return c

    lax.fori_loop(0, ze - 1, faces_z, 0)
    gz_s[ze - 1] = jnp.zeros((ye, xe), jnp.float32)

    def faces(l, c):
        cc = cond_s[l]
        gx = harm(cc, pltpu.roll(cc, xe - 1, 1))
        gx = jnp.where(lane == xe - 1, 0.0, gx)
        gy = harm(cc, pltpu.roll(cc, ye - 1, 0))
        gy = jnp.where(row == ye - 1, 0.0, gy)
        gxl = pltpu.roll(gx, 1, 1)
        gyu = pltpu.roll(gy, 1, 0)
        gx_s[l] = gx
        gxl_s[l] = gxl
        gy_s[l] = gy
        gyu_s[l] = gyu
        lm = jnp.maximum(l - 1, 0)
        gzm = jnp.where(l > 0, gz_s[lm], 0.0)
        sink = jnp.where(z0 + l == 0, SINK_CONDUCT, 0.0)
        diag = inv_s[l] + (gz_s[l] + gzm + gx + gxl + gy + gyu) + sink
        inv_s[l] = 1.0 / diag
        return c

    lax.fori_loop(0, ze, faces, 0)

    def relax(src, l):
        t = t_s[src, l]
        coupled = (gz_s[l] * t_s[src, l + 1] + gz_s[l - 1] * t_s[src, l - 1]
                   + gx_s[l] * pltpu.roll(t, xe - 1, 1) + gxl_s[l] * pltpu.roll(t, 1, 1)
                   + gy_s[l] * pltpu.roll(t, ye - 1, 0) + gyu_s[l] * pltpu.roll(t, 1, 0))
        return (rhs_s[l] + coupled) * inv_s[l]

    for k in range(1, SWEEPS):
        src, dst = (k - 1) % 2, k % 2

        def body(l, c, src=src, dst=dst):
            t_s[dst, l] = relax(src, l)
            return c

        lax.fori_loop(k, ze - k, body, 0)

    last = (SWEEPS - 1) % 2

    def final(i, c):
        new = relax(last, HALO + i)
        out_ref[i] = new[PAD_Y:PAD_Y + strip].T
        return c

    lax.fori_loop(0, local_depth, final, 0)


def local(temp_old, material, conduct_table, capacity_table, dyn_power, leak_ref, die_layer):
    temp_start = temp_old[:, 0]
    cells_mat = material[:, 0]
    local_depth, nx, strip = temp_start.shape
    depth_n = lax.axis_size("depth")
    lat_n = lax.axis_size("lat")
    dies = dyn_power.shape[0] * depth_n
    nz = local_depth * depth_n
    g = lax.axis_index("depth")
    s = lax.axis_index("lat")
    first_layer = g * local_depth
    ye = PAD_Y + strip + HALO + (-(PAD_Y + strip + HALO)) % 8

    tb = from_behind(temp_start[local_depth - HALO:], "depth", 1)
    mb = from_behind(cells_mat[local_depth - HALO:], "depth", 1)
    ta = from_behind(temp_start[:HALO], "depth", -1)
    ma = from_behind(cells_mat[:HALO], "depth", -1)

    def cols(sl):
        parts = [temp_start[:, :, sl], cells_mat[:, :, sl].astype(jnp.float32),
                 dyn_power[:, 0, :, sl], leak_ref[:, 0, :, sl]]
        return jnp.transpose(jnp.concatenate(parts), (0, 2, 1))

    nf = 2 * local_depth + 2
    ylo = from_behind(cols(slice(strip - HALO, strip)), "lat", 1)
    yhi = from_behind(cols(slice(0, HALO)), "lat", -1)

    def widen(centre, lo, hi):
        return jnp.concatenate([jnp.zeros((PAD_Y - HALO, nx), jnp.float32), lo, centre, hi,
                                jnp.zeros((ye - (PAD_Y + strip + HALO), nx), jnp.float32)])

    side = jnp.concatenate([ylo[:2 * local_depth].reshape(2, local_depth, HALO, nx),
                            yhi[:2 * local_depth].reshape(2, local_depth, HALO, nx)], axis=2)
    cb = from_behind(side[:, local_depth - HALO:], "depth", 1)
    ca = from_behind(side[:, :HALO], "depth", -1)

    def pick(die):
        at = die_layer[die] - first_layer
        atc = jnp.clip(at, 0, local_depth - 1)
        layer = widen(lax.dynamic_index_in_dim(temp_start, atc, 0, keepdims=False).T,
                      lax.dynamic_index_in_dim(ylo, atc, 0, keepdims=False),
                      lax.dynamic_index_in_dim(yhi, atc, 0, keepdims=False))
        return jnp.where((at >= 0) & (at < local_depth), layer, 0.0)

    die_temp = pick(g)
    for o in range(1, dies):
        route = [(i, (i + o) % depth_n) for i in range(depth_n)]
        die_temp = die_temp + lax.ppermute(pick((g + o) % dies), "depth", route)
    dyn_w = widen(dyn_power[0, 0].T, ylo[nf - 2], yhi[nf - 2])
    leak_w = widen(leak_ref[0, 0].T, ylo[nf - 1], yhi[nf - 1])
    power_w = dyn_w + leak_w * jnp.exp(LEAK_SLOPE * die_temp)
    die_power = power_w[PAD_Y:PAD_Y + strip].T[None]

    slots = [power_w]
    for o in range(1, dies):
        route = [(i, (i + o) % depth_n) for i in range(depth_n)]
        slots.append(lax.ppermute(power_w, "depth", route))

    sc = jnp.concatenate([jnp.stack([g, s]).astype(jnp.int32), die_layer.astype(jnp.int32)])
    ze = local_depth + 2 * HALO
    smem = pl.BlockSpec(memory_space=pltpu.MemorySpace.SMEM)
    vmem = pl.BlockSpec(memory_space=pltpu.MemorySpace.VMEM)
    full = (ze, ye, nx)
    kern = functools.partial(sweep_kernel, nz, strip * lat_n, local_depth, strip)
    out = pl.pallas_call(
        kern,
        out_shape=jax.ShapeDtypeStruct((local_depth, nx, strip), jnp.float32),
        in_specs=[smem] * 3 + [vmem] * 14,
        out_specs=vmem,
        scratch_shapes=([pltpu.VMEM((2,) + full, jnp.float32)] + [pltpu.VMEM(full, jnp.float32)] * 8),
        compiler_params=pltpu.CompilerParams(vmem_limit_bytes=60 * 1024 * 1024),
        interpret=INTERPRET,
    )(sc, conduct_table, capacity_table, temp_start, cells_mat, tb, mb, ta, ma, ylo, yhi, cb, ca, *slots)
    return (out[:, None], die_power[:, None])


def solution(mesh):
    return jax.shard_map(
        local,
        mesh=mesh,
        in_specs=(
            P("depth", "lat", None, None),
            P("depth", "lat", None, None),
            P(),
            P(),
            P("depth", "lat", None, None),
            P("depth", "lat", None, None),
            P(),
        ),
        out_specs=(P("depth", "lat", None, None), P("depth", "lat", None, None)),
        check_vma=False,
    )
```

```python
import functools

import jax
import jax.numpy as jnp
from jax import lax
from jax.experimental import pallas as pl
from jax.experimental.pallas import tpu as pltpu
from jax.sharding import PartitionSpec as P


SWEEPS = 6
HALO = SWEEPS
PAD_Y = 8

COND_SLOPE = 0.15
LEAK_SLOPE = 0.5
SINK_CONDUCT = 2.0

INTERPRET = False


def from_behind(block, axis, distance):
    devices = range(lax.axis_size(axis))
    route = [(i - distance, i) for i in devices if i - distance in devices]
    return lax.ppermute(block, axis, route)


def diagonal(block, dg, ds):
    nd, nl = lax.axis_size("depth"), lax.axis_size("lat")
    route = [((g - dg) * nl + (t - ds), g * nl + t) for g in range(nd) for t in range(nl)
             if 0 <= g - dg < nd and 0 <= t - ds < nl]
    return lax.ppermute(block, ("depth", "lat"), route)


def harm(a, b):
    summed = a + b
    return 2.0 * a * b / jnp.where(summed > 0, summed, 1.0)


def material_bits(material):
    hi = material >= 4.0
    rest = material - jnp.where(hi, 4.0, 0.0)
    mid = rest >= 2.0
    lo = (rest - jnp.where(mid, 2.0, 0.0)) >= 1.0
    return hi, mid, lo


def lookup(table_ref, bits):
    hi, mid, lo = bits
    t = [table_ref[i] for i in range(8)]
    low = jnp.where(mid, jnp.where(lo, t[3], t[2]), jnp.where(lo, t[1], t[0]))
    high = jnp.where(mid, jnp.where(lo, t[7], t[6]), jnp.where(lo, t[5], t[4]))
    return jnp.where(hi, high, low)


def sweep_kernel(nz, ny_total, local_depth, strip,
                 sc_ref, ctab_ref, htab_ref, tc_ref, mc_ref, tb_ref, mb_ref, ta_ref, ma_ref,
                 ylo_ref, yhi_ref, cbl_ref, cbh_ref, cal_ref, cah_ref, d0_ref, d1_ref, d2_ref, d3_ref,
                 out_ref, t_s, cond_s, rhs_s, inv_s, gz_s, gx_s, gxl_s, gy_s, gyu_s):
    ze = t_s.shape[1]
    ye = t_s.shape[2]
    xe = t_s.shape[3]
    g = sc_ref[0]
    s = sc_ref[1]
    z0 = g * local_depth - HALO
    row = lax.broadcasted_iota(jnp.int32, (ye, xe), 0)
    lane = lax.broadcasted_iota(jnp.int32, (ye, xe), 1)
    yg = s * strip + row - PAD_Y
    yvalid = (yg >= 0) & (yg < ny_total) & (row >= PAD_Y - HALO) & (row < PAD_Y + strip + HALO)
    top = PAD_Y + strip + HALO
    zlo = jnp.zeros((PAD_Y - HALO, xe), jnp.float32)
    zhi = jnp.zeros((ye - top, xe), jnp.float32)

    def put(dst, centre, lo, hi):
        dst[PAD_Y - HALO:PAD_Y] = lo
        dst[PAD_Y:PAD_Y + strip] = centre
        dst[PAD_Y + strip:top] = hi
        dst[0:PAD_Y - HALO] = zlo
        dst[top:ye] = zhi

    def tables(l, temp_raw, mat_raw, t_lo, t_hi, m_lo, m_hi):
        put(t_s.at[0, l], temp_raw.T, t_lo, t_hi)
        put(cond_s.at[l], mat_raw.T.astype(jnp.float32), m_lo, m_hi)
        temp = t_s[0, l]
        mat = cond_s[l]
        zg = z0 + l
        valid = yvalid & (zg >= 0) & (zg < nz)
        bits = material_bits(mat)
        cval = lookup(ctab_ref, bits)
        hval = lookup(htab_ref, bits)
        cond = jnp.where(valid, cval * jnp.exp(-COND_SLOPE * temp), 0.0)
        cond_s[l] = cond
        inv_s[l] = hval
        rhs_s[l] = hval * temp

    def below(i, c):
        tables(i, tb_ref[i], mb_ref[i], cbl_ref[i], cbh_ref[i], cbl_ref[HALO + i], cbh_ref[HALO + i])
        return c

    def centre(i, c):
        tables(HALO + i, tc_ref[i], mc_ref[i], ylo_ref[i], yhi_ref[i],
               ylo_ref[local_depth + i], yhi_ref[local_depth + i])
        return c

    def above(i, c):
        tables(HALO + local_depth + i, ta_ref[i], ma_ref[i], cal_ref[i], cah_ref[i],
               cal_ref[HALO + i], cah_ref[HALO + i])
        return c

    lax.fori_loop(0, HALO, below, 0)
    lax.fori_loop(0, local_depth, centre, 0)
    lax.fori_loop(0, HALO, above, 0)

    slots = (d0_ref, d1_ref, d2_ref, d3_ref)
    dies = len(slots)
    for o in range(dies):
        rel = sc_ref[2 + (g + dies - o) % dies] - z0
        relc = jnp.clip(rel, 0, ze - 1)

        @pl.when((rel >= 0) & (rel < ze))
        def _():
            rhs_s[relc] = inv_s[relc] * t_s[0, relc] + slots[o][...]

    def faces_z(l, c):
        gz_s[l] = harm(cond_s[l], cond_s[l + 1])
        return c

    lax.fori_loop(0, ze - 1, faces_z, 0)
    gz_s[ze - 1] = jnp.zeros((ye, xe), jnp.float32)

    def faces(l, c):
        cc = cond_s[l]
        gx = harm(cc, pltpu.roll(cc, xe - 1, 1))
        gx = jnp.where(lane == xe - 1, 0.0, gx)
        gy = harm(cc, pltpu.roll(cc, ye - 1, 0))
        gy = jnp.where(row == ye - 1, 0.0, gy)
        gxl = pltpu.roll(gx, 1, 1)
        gyu = pltpu.roll(gy, 1, 0)
        gx_s[l] = gx
        gxl_s[l] = gxl
        gy_s[l] = gy
        gyu_s[l] = gyu
        lm = jnp.maximum(l - 1, 0)
        gzm = jnp.where(l > 0, gz_s[lm], 0.0)
        sink = jnp.where(z0 + l == 0, SINK_CONDUCT, 0.0)
        diag = inv_s[l] + (gz_s[l] + gzm + gx + gxl + gy + gyu) + sink
        inv_s[l] = 1.0 / diag
        return c

    lax.fori_loop(0, ze, faces, 0)

    def relax(src, l):
        t = t_s[src, l]
        coupled = (gz_s[l] * t_s[src, l + 1] + gz_s[l - 1] * t_s[src, l - 1]
                   + gx_s[l] * pltpu.roll(t, xe - 1, 1) + gxl_s[l] * pltpu.roll(t, 1, 1)
                   + gy_s[l] * pltpu.roll(t, ye - 1, 0) + gyu_s[l] * pltpu.roll(t, 1, 0))
        return (rhs_s[l] + coupled) * inv_s[l]

    for k in range(1, SWEEPS):
        src, dst = (k - 1) % 2, k % 2

        def body(l, c, src=src, dst=dst):
            t_s[dst, l] = relax(src, l)
            return c

        lax.fori_loop(k, ze - k, body, 0)

    last = (SWEEPS - 1) % 2

    def final(i, c):
        new = relax(last, HALO + i)
        out_ref[i] = new[PAD_Y:PAD_Y + strip].T
        return c

    lax.fori_loop(0, local_depth, final, 0)


def local_body(temp_old, material, conduct_table, capacity_table, dyn_power, leak_ref, die_layer):
    temp_start = temp_old[:, 0]
    cells_mat = material[:, 0]
    local_depth, nx, strip = temp_start.shape
    depth_n = lax.axis_size("depth")
    lat_n = lax.axis_size("lat")
    dies = dyn_power.shape[0] * depth_n
    nz = local_depth * depth_n
    g = lax.axis_index("depth")
    s = lax.axis_index("lat")
    first_layer = g * local_depth
    ye = PAD_Y + strip + HALO + (-(PAD_Y + strip + HALO)) % 8

    tb = from_behind(temp_start[local_depth - HALO:], "depth", 1)
    mb = from_behind(cells_mat[local_depth - HALO:], "depth", 1)
    ta = from_behind(temp_start[:HALO], "depth", -1)
    ma = from_behind(cells_mat[:HALO], "depth", -1)

    def cols(sl):
        parts = [temp_start[:, :, sl], cells_mat[:, :, sl].astype(jnp.float32),
                 dyn_power[:, 0, :, sl], leak_ref[:, 0, :, sl]]
        return jnp.transpose(jnp.concatenate(parts), (0, 2, 1))

    nf = 2 * local_depth + 2
    last_cols, first_cols = cols(slice(strip - HALO, strip)), cols(slice(0, HALO))
    ylo = from_behind(last_cols, "lat", 1)
    yhi = from_behind(first_cols, "lat", -1)

    def faces_of(c, layers):
        return jnp.concatenate([c[layers], c[local_depth + layers.start:local_depth + layers.stop]])

    top, bottom = slice(local_depth - HALO, local_depth), slice(0, HALO)
    cbl = diagonal(faces_of(last_cols, top), 1, 1)
    cbh = diagonal(faces_of(first_cols, top), 1, -1)
    cal = diagonal(faces_of(last_cols, bottom), -1, 1)
    cah = diagonal(faces_of(first_cols, bottom), -1, -1)

    def widen(centre, lo, hi):
        return jnp.concatenate([jnp.zeros((PAD_Y - HALO, nx), jnp.float32), lo, centre, hi,
                                jnp.zeros((ye - (PAD_Y + strip + HALO), nx), jnp.float32)])

    def pick(die):
        at = die_layer[die] - first_layer
        atc = jnp.clip(at, 0, local_depth - 1)
        layer = widen(lax.dynamic_index_in_dim(temp_start, atc, 0, keepdims=False).T,
                      lax.dynamic_index_in_dim(ylo, atc, 0, keepdims=False),
                      lax.dynamic_index_in_dim(yhi, atc, 0, keepdims=False))
        return jnp.where((at >= 0) & (at < local_depth), layer, 0.0)

    die_temp = pick(g)
    for o in range(1, dies):
        route = [(i, (i + o) % depth_n) for i in range(depth_n)]
        die_temp = die_temp + lax.ppermute(pick((g + o) % dies), "depth", route)
    dyn_w = widen(dyn_power[0, 0].T, ylo[nf - 2], yhi[nf - 2])
    leak_w = widen(leak_ref[0, 0].T, ylo[nf - 1], yhi[nf - 1])
    power_w = dyn_w + leak_w * jnp.exp(LEAK_SLOPE * die_temp)
    die_power = power_w[PAD_Y:PAD_Y + strip].T[None]

    slots = [power_w]
    for o in range(1, dies):
        route = [(i, (i + o) % depth_n) for i in range(depth_n)]
        slots.append(lax.ppermute(power_w, "depth", route))

    sc = jnp.concatenate([jnp.stack([g, s]).astype(jnp.int32), die_layer.astype(jnp.int32)])
    ze = local_depth + 2 * HALO
    smem = pl.BlockSpec(memory_space=pltpu.MemorySpace.SMEM)
    vmem = pl.BlockSpec(memory_space=pltpu.MemorySpace.VMEM)
    full = (ze, ye, nx)
    kern = functools.partial(sweep_kernel, nz, strip * lat_n, local_depth, strip)
    out = pl.pallas_call(
        kern,
        out_shape=jax.ShapeDtypeStruct((local_depth, nx, strip), jnp.float32),
        in_specs=[smem] * 3 + [vmem] * 16,
        out_specs=vmem,
        scratch_shapes=([pltpu.VMEM((2,) + full, jnp.float32)] + [pltpu.VMEM(full, jnp.float32)] * 8),
        compiler_params=pltpu.CompilerParams(vmem_limit_bytes=60 * 1024 * 1024),
        interpret=INTERPRET,
    )(sc, conduct_table, capacity_table, temp_start, cells_mat, tb, mb, ta, ma, ylo, yhi,
      cbl, cbh, cal, cah, *slots)
    return (out[:, None], die_power[:, None])


def solution(mesh):
    return jax.shard_map(
        local_body,
        mesh=mesh,
        in_specs=(
            P("depth", "lat", None, None),
            P("depth", "lat", None, None),
            P(),
            P(),
            P("depth", "lat", None, None),
            P("depth", "lat", None, None),
            P(),
        ),
        out_specs=(P("depth", "lat", None, None), P("depth", "lat", None, None)),
        check_vma=False,
    )
```

```python
import functools

import jax
import jax.numpy as jnp
from jax import lax
from jax.experimental import pallas as pl
from jax.experimental.pallas import tpu as pltpu
from jax.sharding import PartitionSpec as P


SWEEPS = 6
HALO = SWEEPS
PAD_Y = 8

COND_SLOPE = 0.15
LEAK_SLOPE = 0.5
SINK_CONDUCT = 2.0

INTERPRET = False


def from_behind(block, axis, distance):
    devices = range(lax.axis_size(axis))
    route = [(i - distance, i) for i in devices if i - distance in devices]
    return lax.ppermute(block, axis, route)


def harm(a, b):
    summed = a + b
    return 2.0 * a * b / jnp.where(summed > 0, summed, 1.0)


def material_bits(material):
    hi = material >= 4.0
    rest = material - jnp.where(hi, 4.0, 0.0)
    mid = rest >= 2.0
    lo = (rest - jnp.where(mid, 2.0, 0.0)) >= 1.0
    return hi, mid, lo


def lookup(table_ref, bits):
    hi, mid, lo = bits
    t = [table_ref[i] for i in range(8)]
    low = jnp.where(mid, jnp.where(lo, t[3], t[2]), jnp.where(lo, t[1], t[0]))
    high = jnp.where(mid, jnp.where(lo, t[7], t[6]), jnp.where(lo, t[5], t[4]))
    return jnp.where(hi, high, low)


def sweep_kernel(nz, ny_total, local_depth, strip,
                 sc_ref, ctab_ref, htab_ref, tc_ref, mc_ref, tb_ref, mb_ref, ta_ref, ma_ref,
                 ylo_ref, yhi_ref, cb_ref, ca_ref, d0_ref, d1_ref, d2_ref, d3_ref,
                 out_ref, t_s, cond_s, rhs_s, inv_s, gz_s, gx_s, gxl_s, gy_s, gyu_s):
    ze = t_s.shape[1]
    ye = t_s.shape[2]
    xe = t_s.shape[3]
    g = sc_ref[0]
    s = sc_ref[1]
    z0 = g * local_depth - HALO
    row = lax.broadcasted_iota(jnp.int32, (ye, xe), 0)
    lane = lax.broadcasted_iota(jnp.int32, (ye, xe), 1)
    yg = s * strip + row - PAD_Y
    yvalid = (yg >= 0) & (yg < ny_total) & (row >= PAD_Y - HALO) & (row < PAD_Y + strip + HALO)
    top = PAD_Y + strip + HALO
    zlo = jnp.zeros((PAD_Y - HALO, xe), jnp.float32)
    zhi = jnp.zeros((ye - top, xe), jnp.float32)

    def put(dst, centre, lo, hi):
        dst[PAD_Y - HALO:PAD_Y] = lo
        dst[PAD_Y:PAD_Y + strip] = centre
        dst[PAD_Y + strip:top] = hi
        dst[0:PAD_Y - HALO] = zlo
        dst[top:ye] = zhi

    def tables(l, temp_raw, mat_raw, t_lo, t_hi, m_lo, m_hi):
        put(t_s.at[0, l], temp_raw.T, t_lo, t_hi)
        put(cond_s.at[l], mat_raw.T.astype(jnp.float32), m_lo, m_hi)
        temp = t_s[0, l]
        mat = cond_s[l]
        zg = z0 + l
        valid = yvalid & (zg >= 0) & (zg < nz)
        bits = material_bits(mat)
        cval = lookup(ctab_ref, bits)
        hval = lookup(htab_ref, bits)
        cond = jnp.where(valid, cval * jnp.exp(-COND_SLOPE * temp), 0.0)
        cond_s[l] = cond
        inv_s[l] = hval
        rhs_s[l] = hval * temp

    def below(i, c):
        tables(i, tb_ref[i], mb_ref[i], cb_ref[0, i, :HALO], cb_ref[0, i, HALO:],
               cb_ref[1, i, :HALO], cb_ref[1, i, HALO:])
        return c

    def centre(i, c):
        tables(HALO + i, tc_ref[i], mc_ref[i], ylo_ref[i], yhi_ref[i],
               ylo_ref[local_depth + i], yhi_ref[local_depth + i])
        return c

    def above(i, c):
        tables(HALO + local_depth + i, ta_ref[i], ma_ref[i], ca_ref[0, i, :HALO], ca_ref[0, i, HALO:],
               ca_ref[1, i, :HALO], ca_ref[1, i, HALO:])
        return c

    lax.fori_loop(0, HALO, below, 0)
    lax.fori_loop(0, local_depth, centre, 0)
    lax.fori_loop(0, HALO, above, 0)

    slots = (d0_ref, d1_ref, d2_ref, d3_ref)
    dies = len(slots)
    for o in range(dies):
        rel = sc_ref[2 + (g + dies - o) % dies] - z0
        relc = jnp.clip(rel, 0, ze - 1)

        @pl.when((rel >= 0) & (rel < ze))
        def _():
            rhs_s[relc] = inv_s[relc] * t_s[0, relc] + slots[o][...]

    def faces_z(l, c):
        gz_s[l] = harm(cond_s[l], cond_s[l + 1])
        return c

    lax.fori_loop(0, ze - 1, faces_z, 0)
    gz_s[ze - 1] = jnp.zeros((ye, xe), jnp.float32)

    def faces(l, c):
        cc = cond_s[l]
        gx = harm(cc, pltpu.roll(cc, xe - 1, 1))
        gx = jnp.where(lane == xe - 1, 0.0, gx)
        gy = harm(cc, pltpu.roll(cc, ye - 1, 0))
        gy = jnp.where(row == ye - 1, 0.0, gy)
        gxl = pltpu.roll(gx, 1, 1)
        gyu = pltpu.roll(gy, 1, 0)
        gx_s[l] = gx
        gxl_s[l] = gxl
        gy_s[l] = gy
        gyu_s[l] = gyu
        lm = jnp.maximum(l - 1, 0)
        gzm = jnp.where(l > 0, gz_s[lm], 0.0)
        sink = jnp.where(z0 + l == 0, SINK_CONDUCT, 0.0)
        diag = inv_s[l] + (gz_s[l] + gzm + gx + gxl + gy + gyu) + sink
        inv_s[l] = 1.0 / diag
        return c

    lax.fori_loop(0, ze, faces, 0)

    def relax(src, l):
        t = t_s[src, l]
        coupled = (gz_s[l] * t_s[src, l + 1] + gz_s[l - 1] * t_s[src, l - 1]
                   + gx_s[l] * pltpu.roll(t, xe - 1, 1) + gxl_s[l] * pltpu.roll(t, 1, 1)
                   + gy_s[l] * pltpu.roll(t, ye - 1, 0) + gyu_s[l] * pltpu.roll(t, 1, 0))
        return (rhs_s[l] + coupled) * inv_s[l]

    for k in range(1, SWEEPS):
        src, dst = (k - 1) % 2, k % 2

        def body(l, c, src=src, dst=dst):
            t_s[dst, l] = relax(src, l)
            return c

        lax.fori_loop(k, ze - k, body, 0)

    last = (SWEEPS - 1) % 2

    def final(i, c):
        new = relax(last, HALO + i)
        out_ref[i] = new[PAD_Y:PAD_Y + strip].T
        return c

    lax.fori_loop(0, local_depth, final, 0)


def local_body(temp_old, material, conduct_table, capacity_table, dyn_power, leak_ref, die_layer):
    temp_start = temp_old[:, 0]
    cells_mat = material[:, 0]
    local_depth, nx, strip = temp_start.shape
    depth_n = lax.axis_size("depth")
    lat_n = lax.axis_size("lat")
    dies = dyn_power.shape[0] * depth_n
    nz = local_depth * depth_n
    g = lax.axis_index("depth")
    s = lax.axis_index("lat")
    first_layer = g * local_depth
    ye = PAD_Y + strip + HALO + (-(PAD_Y + strip + HALO)) % 8

    tb = from_behind(temp_start[local_depth - HALO:], "depth", 1)
    mb = from_behind(cells_mat[local_depth - HALO:], "depth", 1)
    ta = from_behind(temp_start[:HALO], "depth", -1)
    ma = from_behind(cells_mat[:HALO], "depth", -1)

    def cols(sl):
        parts = [temp_start[:, :, sl], cells_mat[:, :, sl].astype(jnp.float32),
                 dyn_power[:, 0, :, sl], leak_ref[:, 0, :, sl]]
        return jnp.transpose(jnp.concatenate(parts), (0, 2, 1))

    nf = 2 * local_depth + 2
    ylo = from_behind(cols(slice(strip - HALO, strip)), "lat", 1)
    yhi = from_behind(cols(slice(0, HALO)), "lat", -1)

    def widen(centre, lo, hi):
        return jnp.concatenate([jnp.zeros((PAD_Y - HALO, nx), jnp.float32), lo, centre, hi,
                                jnp.zeros((ye - (PAD_Y + strip + HALO), nx), jnp.float32)])

    side = jnp.concatenate([ylo[:2 * local_depth].reshape(2, local_depth, HALO, nx),
                            yhi[:2 * local_depth].reshape(2, local_depth, HALO, nx)], axis=2)
    corner_of = {1: side[:, local_depth - HALO:], dies - 1: side[:, :HALO]}

    def pick(die):
        at = die_layer[die] - first_layer
        atc = jnp.clip(at, 0, local_depth - 1)
        layer = widen(lax.dynamic_index_in_dim(temp_start, atc, 0, keepdims=False).T,
                      lax.dynamic_index_in_dim(ylo, atc, 0, keepdims=False),
                      lax.dynamic_index_in_dim(yhi, atc, 0, keepdims=False))
        return jnp.where((at >= 0) & (at < local_depth), layer, 0.0)

    die_temp = pick(g)
    got_corners = {}
    for o in range(1, dies):
        route = [(i, (i + o) % depth_n) for i in range(depth_n)]
        sent = pick((g + o) % dies)
        if o in corner_of:
            sent = jnp.concatenate([sent, corner_of[o].reshape(-1, nx)])
        got = lax.ppermute(sent, "depth", route)
        die_temp = die_temp + got[:ye]
        if o in corner_of:
            got_corners[o] = got[ye:].reshape(2, HALO, 2 * HALO, nx)
    cb, ca = got_corners[1], got_corners[dies - 1]
    dyn_w = widen(dyn_power[0, 0].T, ylo[nf - 2], yhi[nf - 2])
    leak_w = widen(leak_ref[0, 0].T, ylo[nf - 1], yhi[nf - 1])
    power_w = dyn_w + leak_w * jnp.exp(LEAK_SLOPE * die_temp)
    die_power = power_w[PAD_Y:PAD_Y + strip].T[None]

    slots = [power_w]
    for o in range(1, dies):
        route = [(i, (i + o) % depth_n) for i in range(depth_n)]
        slots.append(lax.ppermute(power_w, "depth", route))

    sc = jnp.concatenate([jnp.stack([g, s]).astype(jnp.int32), die_layer.astype(jnp.int32)])
    ze = local_depth + 2 * HALO
    smem = pl.BlockSpec(memory_space=pltpu.MemorySpace.SMEM)
    vmem = pl.BlockSpec(memory_space=pltpu.MemorySpace.VMEM)
    full = (ze, ye, nx)
    kern = functools.partial(sweep_kernel, nz, strip * lat_n, local_depth, strip)
    out = pl.pallas_call(
        kern,
        out_shape=jax.ShapeDtypeStruct((local_depth, nx, strip), jnp.float32),
        in_specs=[smem] * 3 + [vmem] * 14,
        out_specs=vmem,
        scratch_shapes=([pltpu.VMEM((2,) + full, jnp.float32)] + [pltpu.VMEM(full, jnp.float32)] * 8),
        compiler_params=pltpu.CompilerParams(vmem_limit_bytes=60 * 1024 * 1024),
        interpret=INTERPRET,
    )(sc, conduct_table, capacity_table, temp_start, cells_mat, tb, mb, ta, ma, ylo, yhi, cb, ca, *slots)
    return (out[:, None], die_power[:, None])


def solution(mesh):
    return jax.shard_map(
        local_body,
        mesh=mesh,
        in_specs=(
            P("depth", "lat", None, None),
            P("depth", "lat", None, None),
            P(),
            P(),
            P("depth", "lat", None, None),
            P("depth", "lat", None, None),
            P(),
        ),
        out_specs=(P("depth", "lat", None, None), P("depth", "lat", None, None)),
        check_vma=False,
    )
```

```python
import functools

import jax
import jax.numpy as jnp
from jax import lax
from jax.experimental import pallas as pl
from jax.experimental.pallas import tpu as pltpu
from jax.sharding import PartitionSpec as P


SWEEPS = 6
HALO = SWEEPS
PAD_Y = 8

COND_SLOPE = 0.15
LEAK_SLOPE = 0.5
SINK_CONDUCT = 2.0

INTERPRET = False


def from_behind(block, axis, distance):
    devices = range(lax.axis_size(axis))
    route = [(i - distance, i) for i in devices if i - distance in devices]
    return lax.ppermute(block, axis, route)


def harm(a, b):
    summed = a + b
    return 2.0 * a * b / jnp.where(summed > 0, summed, 1.0)


def material_bits(material):
    hi = material >= 4.0
    rest = material - jnp.where(hi, 4.0, 0.0)
    mid = rest >= 2.0
    lo = (rest - jnp.where(mid, 2.0, 0.0)) >= 1.0
    return hi, mid, lo


def lookup(table_ref, bits):
    hi, mid, lo = bits
    t = [table_ref[i] for i in range(8)]
    low = jnp.where(mid, jnp.where(lo, t[3], t[2]), jnp.where(lo, t[1], t[0]))
    high = jnp.where(mid, jnp.where(lo, t[7], t[6]), jnp.where(lo, t[5], t[4]))
    return jnp.where(hi, high, low)


def sweep_kernel(nz, ny_total, local_depth, strip,
                 sc_ref, ctab_ref, htab_ref, tc_ref, mc_ref, tb_ref, mb_ref, ta_ref, ma_ref,
                 ylo_ref, yhi_ref, cb_ref, ca_ref, d0_ref, d1_ref, d2_ref, d3_ref,
                 out_ref, t_s, cond_s, rhs_s, inv_s, gz_s, gx_s, gxl_s, gy_s, gyu_s):
    ze = t_s.shape[1]
    ye = t_s.shape[2]
    xe = t_s.shape[3]
    g = sc_ref[0]
    s = sc_ref[1]
    z0 = g * local_depth - HALO
    row = lax.broadcasted_iota(jnp.int32, (ye, xe), 0)
    lane = lax.broadcasted_iota(jnp.int32, (ye, xe), 1)
    yg = s * strip + row - PAD_Y
    yvalid = (yg >= 0) & (yg < ny_total) & (row >= PAD_Y - HALO) & (row < PAD_Y + strip + HALO)
    top = PAD_Y + strip + HALO
    zlo = jnp.zeros((PAD_Y - HALO, xe), jnp.float32)
    zhi = jnp.zeros((ye - top, xe), jnp.float32)

    def put(dst, centre, lo, hi):
        dst[PAD_Y - HALO:PAD_Y] = lo
        dst[PAD_Y:PAD_Y + strip] = centre
        dst[PAD_Y + strip:top] = hi
        dst[0:PAD_Y - HALO] = zlo
        dst[top:ye] = zhi

    def tables(l, temp_raw, mat_raw, t_lo, t_hi, m_lo, m_hi):
        put(t_s.at[0, l], temp_raw.T, t_lo, t_hi)
        put(cond_s.at[l], mat_raw.T.astype(jnp.float32), m_lo, m_hi)
        temp = t_s[0, l]
        mat = cond_s[l]
        zg = z0 + l
        valid = yvalid & (zg >= 0) & (zg < nz)
        bits = material_bits(mat)
        cval = lookup(ctab_ref, bits)
        hval = lookup(htab_ref, bits)
        cond = jnp.where(valid, cval * jnp.exp(-COND_SLOPE * temp), 0.0)
        cond_s[l] = cond
        inv_s[l] = hval
        rhs_s[l] = hval * temp

    def below(i, c):
        tables(i, tb_ref[i], mb_ref[i], cb_ref[0, i, :HALO], cb_ref[0, i, HALO:],
               cb_ref[1, i, :HALO], cb_ref[1, i, HALO:])
        return c

    def centre(i, c):
        tables(HALO + i, tc_ref[i], mc_ref[i], ylo_ref[i], yhi_ref[i],
               ylo_ref[local_depth + i], yhi_ref[local_depth + i])
        return c

    def above(i, c):
        tables(HALO + local_depth + i, ta_ref[i], ma_ref[i], ca_ref[0, i, :HALO], ca_ref[0, i, HALO:],
               ca_ref[1, i, :HALO], ca_ref[1, i, HALO:])
        return c

    lax.fori_loop(0, HALO, below, 0)
    lax.fori_loop(0, local_depth, centre, 0)
    lax.fori_loop(0, HALO, above, 0)

    slots = (d0_ref, d1_ref, d2_ref, d3_ref)
    dies = len(slots)
    for o in range(dies):
        rel = sc_ref[2 + (g + dies - o) % dies] - z0
        relc = jnp.clip(rel, 0, ze - 1)

        @pl.when((rel >= 0) & (rel < ze))
        def _():
            rhs_s[relc] = inv_s[relc] * t_s[0, relc] + slots[o][...]

    def faces_z(l, c):
        gz_s[l] = harm(cond_s[l], cond_s[l + 1])
        return c

    lax.fori_loop(0, ze - 1, faces_z, 0)
    gz_s[ze - 1] = jnp.zeros((ye, xe), jnp.float32)

    def faces(l, c):
        cc = cond_s[l]
        gx = harm(cc, pltpu.roll(cc, xe - 1, 1))
        gx = jnp.where(lane == xe - 1, 0.0, gx)
        gy = harm(cc, pltpu.roll(cc, ye - 1, 0))
        gy = jnp.where(row == ye - 1, 0.0, gy)
        gxl = pltpu.roll(gx, 1, 1)
        gyu = pltpu.roll(gy, 1, 0)
        gx_s[l] = gx
        gxl_s[l] = gxl
        gy_s[l] = gy
        gyu_s[l] = gyu
        lm = jnp.maximum(l - 1, 0)
        gzm = jnp.where(l > 0, gz_s[lm], 0.0)
        sink = jnp.where(z0 + l == 0, SINK_CONDUCT, 0.0)
        diag = inv_s[l] + (gz_s[l] + gzm + gx + gxl + gy + gyu) + sink
        inv_s[l] = 1.0 / diag
        return c

    lax.fori_loop(1, ze - 1, faces, 0)

    def relax(src, l):
        t = t_s[src, l]
        coupled = (gz_s[l] * t_s[src, l + 1] + gz_s[l - 1] * t_s[src, l - 1]
                   + gx_s[l] * pltpu.roll(t, xe - 1, 1) + gxl_s[l] * pltpu.roll(t, 1, 1)
                   + gy_s[l] * pltpu.roll(t, ye - 1, 0) + gyu_s[l] * pltpu.roll(t, 1, 0))
        return (rhs_s[l] + coupled) * inv_s[l]

    for k in range(1, SWEEPS):
        src, dst = (k - 1) % 2, k % 2

        def body(l, c, src=src, dst=dst):
            t_s[dst, l] = relax(src, l)
            return c

        lax.fori_loop(k, ze - k, body, 0)

    last = (SWEEPS - 1) % 2

    def final(i, c):
        new = relax(last, HALO + i)
        out_ref[i] = new[PAD_Y:PAD_Y + strip].T
        return c

    lax.fori_loop(0, local_depth, final, 0)


def local_body(temp_old, material, conduct_table, capacity_table, dyn_power, leak_ref, die_layer):
    temp_start = temp_old[:, 0]
    cells_mat = material[:, 0]
    local_depth, nx, strip = temp_start.shape
    depth_n = lax.axis_size("depth")
    lat_n = lax.axis_size("lat")
    dies = dyn_power.shape[0] * depth_n
    nz = local_depth * depth_n
    g = lax.axis_index("depth")
    s = lax.axis_index("lat")
    first_layer = g * local_depth
    ye = PAD_Y + strip + HALO + (-(PAD_Y + strip + HALO)) % 8

    tb = from_behind(temp_start[local_depth - HALO:], "depth", 1)
    mb = from_behind(cells_mat[local_depth - HALO:], "depth", 1)
    ta = from_behind(temp_start[:HALO], "depth", -1)
    ma = from_behind(cells_mat[:HALO], "depth", -1)

    def cols(sl):
        parts = [temp_start[:, :, sl], cells_mat[:, :, sl].astype(jnp.float32),
                 dyn_power[:, 0, :, sl], leak_ref[:, 0, :, sl]]
        return jnp.transpose(jnp.concatenate(parts), (0, 2, 1))

    nf = 2 * local_depth + 2
    ylo = from_behind(cols(slice(strip - HALO, strip)), "lat", 1)
    yhi = from_behind(cols(slice(0, HALO)), "lat", -1)

    def widen(centre, lo, hi):
        return jnp.concatenate([jnp.zeros((PAD_Y - HALO, nx), jnp.float32), lo, centre, hi,
                                jnp.zeros((ye - (PAD_Y + strip + HALO), nx), jnp.float32)])

    side = jnp.concatenate([ylo[:2 * local_depth].reshape(2, local_depth, HALO, nx),
                            yhi[:2 * local_depth].reshape(2, local_depth, HALO, nx)], axis=2)
    cb = from_behind(side[:, local_depth - HALO:], "depth", 1)
    ca = from_behind(side[:, :HALO], "depth", -1)

    def pick(die):
        at = die_layer[die] - first_layer
        atc = jnp.clip(at, 0, local_depth - 1)
        layer = widen(lax.dynamic_index_in_dim(temp_start, atc, 0, keepdims=False).T,
                      lax.dynamic_index_in_dim(ylo, atc, 0, keepdims=False),
                      lax.dynamic_index_in_dim(yhi, atc, 0, keepdims=False))
        return jnp.where((at >= 0) & (at < local_depth), layer, 0.0)

    die_temp = pick(g)
    for o in range(1, dies):
        route = [(i, (i + o) % depth_n) for i in range(depth_n)]
        die_temp = die_temp + lax.ppermute(pick((g + o) % dies), "depth", route)
    dyn_w = widen(dyn_power[0, 0].T, ylo[nf - 2], yhi[nf - 2])
    leak_w = widen(leak_ref[0, 0].T, ylo[nf - 1], yhi[nf - 1])
    power_w = dyn_w + leak_w * jnp.exp(LEAK_SLOPE * die_temp)
    die_power = power_w[PAD_Y:PAD_Y + strip].T[None]

    slots = [power_w]
    for o in range(1, dies):
        route = [(i, (i + o) % depth_n) for i in range(depth_n)]
        slots.append(lax.ppermute(power_w, "depth", route))

    sc = jnp.concatenate([jnp.stack([g, s]).astype(jnp.int32), die_layer.astype(jnp.int32)])
    ze = local_depth + 2 * HALO
    smem = pl.BlockSpec(memory_space=pltpu.MemorySpace.SMEM)
    vmem = pl.BlockSpec(memory_space=pltpu.MemorySpace.VMEM)
    full = (ze, ye, nx)
    kern = functools.partial(sweep_kernel, nz, strip * lat_n, local_depth, strip)
    out = pl.pallas_call(
        kern,
        out_shape=jax.ShapeDtypeStruct((local_depth, nx, strip), jnp.float32),
        in_specs=[smem] * 3 + [vmem] * 14,
        out_specs=vmem,
        scratch_shapes=([pltpu.VMEM((2,) + full, jnp.float32)] + [pltpu.VMEM(full, jnp.float32)] * 8),
        compiler_params=pltpu.CompilerParams(vmem_limit_bytes=60 * 1024 * 1024),
        interpret=INTERPRET,
    )(sc, conduct_table, capacity_table, temp_start, cells_mat, tb, mb, ta, ma, ylo, yhi, cb, ca, *slots)
    return (out[:, None], die_power[:, None])


def solution(mesh):
    return jax.shard_map(
        local_body,
        mesh=mesh,
        in_specs=(
            P("depth", "lat", None, None),
            P("depth", "lat", None, None),
            P(),
            P(),
            P("depth", "lat", None, None),
            P("depth", "lat", None, None),
            P(),
        ),
        out_specs=(P("depth", "lat", None, None), P("depth", "lat", None, None)),
        check_vma=False,
    )
```

```python
import functools

import jax
import jax.numpy as jnp
from jax import lax
from jax.experimental import pallas as pl
from jax.experimental.pallas import tpu as pltpu
from jax.sharding import PartitionSpec as P


SWEEPS = 6
HALO = SWEEPS
PAD_Y = 8

COND_SLOPE = 0.15
LEAK_SLOPE = 0.5
SINK_CONDUCT = 2.0

INTERPRET = False


def from_behind(block, axis, distance):
    devices = range(lax.axis_size(axis))
    route = [(i - distance, i) for i in devices if i - distance in devices]
    return lax.ppermute(block, axis, route)


def halo_copy_kernel(halo, t_hbm, m_hbm, tb_o, mb_o, ta_o, ma_o, sems):
    depth = t_hbm.shape[0]
    copies = [pltpu.make_async_copy(t_hbm.at[pl.ds(depth - halo, halo)], tb_o, sems.at[0]),
              pltpu.make_async_copy(m_hbm.at[pl.ds(depth - halo, halo)], mb_o, sems.at[1]),
              pltpu.make_async_copy(t_hbm.at[pl.ds(0, halo)], ta_o, sems.at[2]),
              pltpu.make_async_copy(m_hbm.at[pl.ds(0, halo)], ma_o, sems.at[3])]
    for c in copies:
        c.start()
    for c in copies:
        c.wait()


def halo_slices(temp, mat):
    shape = (HALO,) + temp.shape[1:]
    anyspec = pl.BlockSpec(memory_space=pl.ANY)
    return pl.pallas_call(
        functools.partial(halo_copy_kernel, HALO),
        out_shape=[jax.ShapeDtypeStruct(shape, temp.dtype), jax.ShapeDtypeStruct(shape, mat.dtype)] * 2,
        in_specs=[anyspec, anyspec],
        out_specs=[anyspec] * 4,
        scratch_shapes=[pltpu.SemaphoreType.DMA((4,))],
        interpret=INTERPRET,
    )(temp, mat)


def harm(a, b):
    summed = a + b
    return 2.0 * a * b / jnp.where(summed > 0, summed, 1.0)


def material_bits(material):
    hi = material >= 4.0
    rest = material - jnp.where(hi, 4.0, 0.0)
    mid = rest >= 2.0
    lo = (rest - jnp.where(mid, 2.0, 0.0)) >= 1.0
    return hi, mid, lo


def lookup(table_ref, bits):
    hi, mid, lo = bits
    t = [table_ref[i] for i in range(8)]
    low = jnp.where(mid, jnp.where(lo, t[3], t[2]), jnp.where(lo, t[1], t[0]))
    high = jnp.where(mid, jnp.where(lo, t[7], t[6]), jnp.where(lo, t[5], t[4]))
    return jnp.where(hi, high, low)


def sweep_kernel(nz, ny_total, local_depth, strip,
                 sc_ref, ctab_ref, htab_ref, tc_ref, mc_ref, tb_ref, mb_ref, ta_ref, ma_ref,
                 ylo_ref, yhi_ref, cb_ref, ca_ref, d0_ref, d1_ref, d2_ref, d3_ref,
                 out_ref, t_s, cond_s, rhs_s, inv_s, gz_s, gx_s, gxl_s, gy_s, gyu_s):
    ze = t_s.shape[1]
    ye = t_s.shape[2]
    xe = t_s.shape[3]
    g = sc_ref[0]
    s = sc_ref[1]
    z0 = g * local_depth - HALO
    row = lax.broadcasted_iota(jnp.int32, (ye, xe), 0)
    lane = lax.broadcasted_iota(jnp.int32, (ye, xe), 1)
    yg = s * strip + row - PAD_Y
    yvalid = (yg >= 0) & (yg < ny_total) & (row >= PAD_Y - HALO) & (row < PAD_Y + strip + HALO)
    top = PAD_Y + strip + HALO
    zlo = jnp.zeros((PAD_Y - HALO, xe), jnp.float32)
    zhi = jnp.zeros((ye - top, xe), jnp.float32)

    def put(dst, centre, lo, hi):
        dst[PAD_Y - HALO:PAD_Y] = lo
        dst[PAD_Y:PAD_Y + strip] = centre
        dst[PAD_Y + strip:top] = hi
        dst[0:PAD_Y - HALO] = zlo
        dst[top:ye] = zhi

    def tables(l, temp_raw, mat_raw, t_lo, t_hi, m_lo, m_hi):
        put(t_s.at[0, l], temp_raw.T, t_lo, t_hi)
        put(cond_s.at[l], mat_raw.T.astype(jnp.float32), m_lo, m_hi)
        temp = t_s[0, l]
        mat = cond_s[l]
        zg = z0 + l
        valid = yvalid & (zg >= 0) & (zg < nz)
        bits = material_bits(mat)
        cval = lookup(ctab_ref, bits)
        hval = lookup(htab_ref, bits)
        cond = jnp.where(valid, cval * jnp.exp(-COND_SLOPE * temp), 0.0)
        cond_s[l] = cond
        inv_s[l] = hval
        rhs_s[l] = hval * temp

    def below(i, c):
        tables(i, tb_ref[i], mb_ref[i], cb_ref[0, i, :HALO], cb_ref[0, i, HALO:],
               cb_ref[1, i, :HALO], cb_ref[1, i, HALO:])
        return c

    def centre(i, c):
        tables(HALO + i, tc_ref[i], mc_ref[i], ylo_ref[i], yhi_ref[i],
               ylo_ref[local_depth + i], yhi_ref[local_depth + i])
        return c

    def above(i, c):
        tables(HALO + local_depth + i, ta_ref[i], ma_ref[i], ca_ref[0, i, :HALO], ca_ref[0, i, HALO:],
               ca_ref[1, i, :HALO], ca_ref[1, i, HALO:])
        return c

    lax.fori_loop(0, HALO, below, 0)
    lax.fori_loop(0, local_depth, centre, 0)
    lax.fori_loop(0, HALO, above, 0)

    slots = (d0_ref, d1_ref, d2_ref, d3_ref)
    dies = len(slots)
    for o in range(dies):
        rel = sc_ref[2 + (g + dies - o) % dies] - z0
        relc = jnp.clip(rel, 0, ze - 1)

        @pl.when((rel >= 0) & (rel < ze))
        def _():
            rhs_s[relc] = inv_s[relc] * t_s[0, relc] + slots[o][...]

    def faces_z(l, c):
        gz_s[l] = harm(cond_s[l], cond_s[l + 1])
        return c

    lax.fori_loop(0, ze - 1, faces_z, 0)
    gz_s[ze - 1] = jnp.zeros((ye, xe), jnp.float32)

    def faces(l, c):
        cc = cond_s[l]
        gx = harm(cc, pltpu.roll(cc, xe - 1, 1))
        gx = jnp.where(lane == xe - 1, 0.0, gx)
        gy = harm(cc, pltpu.roll(cc, ye - 1, 0))
        gy = jnp.where(row == ye - 1, 0.0, gy)
        gxl = pltpu.roll(gx, 1, 1)
        gyu = pltpu.roll(gy, 1, 0)
        gx_s[l] = gx
        gxl_s[l] = gxl
        gy_s[l] = gy
        gyu_s[l] = gyu
        lm = jnp.maximum(l - 1, 0)
        gzm = jnp.where(l > 0, gz_s[lm], 0.0)
        sink = jnp.where(z0 + l == 0, SINK_CONDUCT, 0.0)
        diag = inv_s[l] + (gz_s[l] + gzm + gx + gxl + gy + gyu) + sink
        inv_s[l] = 1.0 / diag
        return c

    lax.fori_loop(1, ze - 1, faces, 0)

    def relax(src, l):
        t = t_s[src, l]
        coupled = (gz_s[l] * t_s[src, l + 1] + gz_s[l - 1] * t_s[src, l - 1]
                   + gx_s[l] * pltpu.roll(t, xe - 1, 1) + gxl_s[l] * pltpu.roll(t, 1, 1)
                   + gy_s[l] * pltpu.roll(t, ye - 1, 0) + gyu_s[l] * pltpu.roll(t, 1, 0))
        return (rhs_s[l] + coupled) * inv_s[l]

    for k in range(1, SWEEPS):
        src, dst = (k - 1) % 2, k % 2

        def body(l, c, src=src, dst=dst):
            t_s[dst, l] = relax(src, l)
            return c

        lax.fori_loop(k, ze - k, body, 0)

    last = (SWEEPS - 1) % 2

    def final(i, c):
        new = relax(last, HALO + i)
        out_ref[i] = new[PAD_Y:PAD_Y + strip].T
        return c

    lax.fori_loop(0, local_depth, final, 0)


def local_body(temp_old, material, conduct_table, capacity_table, dyn_power, leak_ref, die_layer):
    temp_start = temp_old[:, 0]
    cells_mat = material[:, 0]
    local_depth, nx, strip = temp_start.shape
    depth_n = lax.axis_size("depth")
    lat_n = lax.axis_size("lat")
    dies = dyn_power.shape[0] * depth_n
    nz = local_depth * depth_n
    g = lax.axis_index("depth")
    s = lax.axis_index("lat")
    first_layer = g * local_depth
    ye = PAD_Y + strip + HALO + (-(PAD_Y + strip + HALO)) % 8

    top_t, top_m, bottom_t, bottom_m = halo_slices(temp_start, cells_mat)
    tb = from_behind(top_t, "depth", 1)
    mb = from_behind(top_m, "depth", 1)
    ta = from_behind(bottom_t, "depth", -1)
    ma = from_behind(bottom_m, "depth", -1)

    def cols(sl):
        parts = [temp_start[:, :, sl], cells_mat[:, :, sl].astype(jnp.float32),
                 dyn_power[:, 0, :, sl], leak_ref[:, 0, :, sl]]
        return jnp.transpose(jnp.concatenate(parts), (0, 2, 1))

    nf = 2 * local_depth + 2
    ylo = from_behind(cols(slice(strip - HALO, strip)), "lat", 1)
    yhi = from_behind(cols(slice(0, HALO)), "lat", -1)

    def widen(centre, lo, hi):
        return jnp.concatenate([jnp.zeros((PAD_Y - HALO, nx), jnp.float32), lo, centre, hi,
                                jnp.zeros((ye - (PAD_Y + strip + HALO), nx), jnp.float32)])

    side = jnp.concatenate([ylo[:2 * local_depth].reshape(2, local_depth, HALO, nx),
                            yhi[:2 * local_depth].reshape(2, local_depth, HALO, nx)], axis=2)
    cb = from_behind(side[:, local_depth - HALO:], "depth", 1)
    ca = from_behind(side[:, :HALO], "depth", -1)

    def pick(die):
        at = die_layer[die] - first_layer
        atc = jnp.clip(at, 0, local_depth - 1)
        layer = widen(lax.dynamic_index_in_dim(temp_start, atc, 0, keepdims=False).T,
                      lax.dynamic_index_in_dim(ylo, atc, 0, keepdims=False),
                      lax.dynamic_index_in_dim(yhi, atc, 0, keepdims=False))
        return jnp.where((at >= 0) & (at < local_depth), layer, 0.0)

    die_temp = pick(g)
    for o in range(1, dies):
        route = [(i, (i + o) % depth_n) for i in range(depth_n)]
        die_temp = die_temp + lax.ppermute(pick((g + o) % dies), "depth", route)
    dyn_w = widen(dyn_power[0, 0].T, ylo[nf - 2], yhi[nf - 2])
    leak_w = widen(leak_ref[0, 0].T, ylo[nf - 1], yhi[nf - 1])
    power_w = dyn_w + leak_w * jnp.exp(LEAK_SLOPE * die_temp)
    die_power = power_w[PAD_Y:PAD_Y + strip].T[None]

    slots = [power_w]
    for o in range(1, dies):
        route = [(i, (i + o) % depth_n) for i in range(depth_n)]
        slots.append(lax.ppermute(power_w, "depth", route))

    sc = jnp.concatenate([jnp.stack([g, s]).astype(jnp.int32), die_layer.astype(jnp.int32)])
    ze = local_depth + 2 * HALO
    smem = pl.BlockSpec(memory_space=pltpu.MemorySpace.SMEM)
    vmem = pl.BlockSpec(memory_space=pltpu.MemorySpace.VMEM)
    full = (ze, ye, nx)
    kern = functools.partial(sweep_kernel, nz, strip * lat_n, local_depth, strip)
    out = pl.pallas_call(
        kern,
        out_shape=jax.ShapeDtypeStruct((local_depth, nx, strip), jnp.float32),
        in_specs=[smem] * 3 + [vmem] * 14,
        out_specs=vmem,
        scratch_shapes=([pltpu.VMEM((2,) + full, jnp.float32)] + [pltpu.VMEM(full, jnp.float32)] * 8),
        compiler_params=pltpu.CompilerParams(vmem_limit_bytes=60 * 1024 * 1024),
        interpret=INTERPRET,
    )(sc, conduct_table, capacity_table, temp_start, cells_mat, tb, mb, ta, ma, ylo, yhi, cb, ca, *slots)
    return (out[:, None], die_power[:, None])


def solution(mesh):
    return jax.shard_map(
        local_body,
        mesh=mesh,
        in_specs=(
            P("depth", "lat", None, None),
            P("depth", "lat", None, None),
            P(),
            P(),
            P("depth", "lat", None, None),
            P("depth", "lat", None, None),
            P(),
        ),
        out_specs=(P("depth", "lat", None, None), P("depth", "lat", None, None)),
        check_vma=False,
    )
```

```python
import functools

import jax
import jax.numpy as jnp
from jax import lax
from jax.experimental import pallas as pl
from jax.experimental.pallas import tpu as pltpu
from jax.sharding import PartitionSpec as P


SWEEPS = 6
HALO = SWEEPS
PAD_Y = 8

COND_SLOPE = 0.15
LEAK_SLOPE = 0.5
SINK_CONDUCT = 2.0

INTERPRET = False


def from_behind(block, axis, distance):
    devices = range(lax.axis_size(axis))
    route = [(i - distance, i) for i in devices if i - distance in devices]
    return lax.ppermute(block, axis, route)


def harm(a, b):
    summed = a + b
    return 2.0 * a * b / jnp.where(summed > 0, summed, 1.0)


def material_bits(material):
    hi = material >= 4.0
    rest = material - jnp.where(hi, 4.0, 0.0)
    mid = rest >= 2.0
    lo = (rest - jnp.where(mid, 2.0, 0.0)) >= 1.0
    return hi, mid, lo


def lookup(table_ref, bits):
    hi, mid, lo = bits
    t = [table_ref[i] for i in range(8)]
    low = jnp.where(mid, jnp.where(lo, t[3], t[2]), jnp.where(lo, t[1], t[0]))
    high = jnp.where(mid, jnp.where(lo, t[7], t[6]), jnp.where(lo, t[5], t[4]))
    return jnp.where(hi, high, low)


def sweep_kernel(nz, ny_total, local_depth, strip,
                 sc_ref, ctab_ref, htab_ref, tc_ref, mc_ref, xb_ref, xa_ref,
                 ylo_ref, yhi_ref, cb_ref, ca_ref, d0_ref, d1_ref, d2_ref, d3_ref,
                 out_ref, t_s, cond_s, rhs_s, inv_s, gz_s, gx_s, gxl_s, gy_s, gyu_s):
    ze = t_s.shape[1]
    ye = t_s.shape[2]
    xe = t_s.shape[3]
    g = sc_ref[0]
    s = sc_ref[1]
    z0 = g * local_depth - HALO
    row = lax.broadcasted_iota(jnp.int32, (ye, xe), 0)
    lane = lax.broadcasted_iota(jnp.int32, (ye, xe), 1)
    yg = s * strip + row - PAD_Y
    yvalid = (yg >= 0) & (yg < ny_total) & (row >= PAD_Y - HALO) & (row < PAD_Y + strip + HALO)
    top = PAD_Y + strip + HALO
    zlo = jnp.zeros((PAD_Y - HALO, xe), jnp.float32)
    zhi = jnp.zeros((ye - top, xe), jnp.float32)

    def put(dst, centre, lo, hi):
        dst[PAD_Y - HALO:PAD_Y] = lo
        dst[PAD_Y:PAD_Y + strip] = centre
        dst[PAD_Y + strip:top] = hi
        dst[0:PAD_Y - HALO] = zlo
        dst[top:ye] = zhi

    def tables(l, temp_raw, mat_raw, t_lo, t_hi, m_lo, m_hi):
        put(t_s.at[0, l], temp_raw.T, t_lo, t_hi)
        put(cond_s.at[l], mat_raw.T.astype(jnp.float32), m_lo, m_hi)
        temp = t_s[0, l]
        mat = cond_s[l]
        zg = z0 + l
        valid = yvalid & (zg >= 0) & (zg < nz)
        bits = material_bits(mat)
        cval = lookup(ctab_ref, bits)
        hval = lookup(htab_ref, bits)
        cond = jnp.where(valid, cval * jnp.exp(-COND_SLOPE * temp), 0.0)
        cond_s[l] = cond
        inv_s[l] = hval
        rhs_s[l] = hval * temp

    def below(i, c):
        tables(i, xb_ref[0, i], xb_ref[1, i], cb_ref[0, i, :HALO], cb_ref[0, i, HALO:],
               cb_ref[1, i, :HALO], cb_ref[1, i, HALO:])
        return c

    def centre(i, c):
        tables(HALO + i, tc_ref[i], mc_ref[i], ylo_ref[i], yhi_ref[i],
               ylo_ref[local_depth + i], yhi_ref[local_depth + i])
        return c

    def above(i, c):
        tables(HALO + local_depth + i, xa_ref[0, i], xa_ref[1, i], ca_ref[0, i, :HALO], ca_ref[0, i, HALO:],
               ca_ref[1, i, :HALO], ca_ref[1, i, HALO:])
        return c

    lax.fori_loop(0, HALO, below, 0)
    lax.fori_loop(0, local_depth, centre, 0)
    lax.fori_loop(0, HALO, above, 0)

    slots = (d0_ref, d1_ref, d2_ref, d3_ref)
    dies = len(slots)
    for o in range(dies):
        rel = sc_ref[2 + (g + dies - o) % dies] - z0
        relc = jnp.clip(rel, 0, ze - 1)

        @pl.when((rel >= 0) & (rel < ze))
        def _():
            rhs_s[relc] = inv_s[relc] * t_s[0, relc] + slots[o][...]

    def faces_z(l, c):
        gz_s[l] = harm(cond_s[l], cond_s[l + 1])
        return c

    lax.fori_loop(0, ze - 1, faces_z, 0)
    gz_s[ze - 1] = jnp.zeros((ye, xe), jnp.float32)

    def faces(l, c):
        cc = cond_s[l]
        gx = harm(cc, pltpu.roll(cc, xe - 1, 1))
        gx = jnp.where(lane == xe - 1, 0.0, gx)
        gy = harm(cc, pltpu.roll(cc, ye - 1, 0))
        gy = jnp.where(row == ye - 1, 0.0, gy)
        gxl = pltpu.roll(gx, 1, 1)
        gyu = pltpu.roll(gy, 1, 0)
        gx_s[l] = gx
        gxl_s[l] = gxl
        gy_s[l] = gy
        gyu_s[l] = gyu
        lm = jnp.maximum(l - 1, 0)
        gzm = jnp.where(l > 0, gz_s[lm], 0.0)
        sink = jnp.where(z0 + l == 0, SINK_CONDUCT, 0.0)
        diag = inv_s[l] + (gz_s[l] + gzm + gx + gxl + gy + gyu) + sink
        inv_s[l] = 1.0 / diag
        return c

    lax.fori_loop(1, ze - 1, faces, 0)

    def relax(src, l):
        t = t_s[src, l]
        coupled = (gz_s[l] * t_s[src, l + 1] + gz_s[l - 1] * t_s[src, l - 1]
                   + gx_s[l] * pltpu.roll(t, xe - 1, 1) + gxl_s[l] * pltpu.roll(t, 1, 1)
                   + gy_s[l] * pltpu.roll(t, ye - 1, 0) + gyu_s[l] * pltpu.roll(t, 1, 0))
        return (rhs_s[l] + coupled) * inv_s[l]

    for k in range(1, SWEEPS):
        src, dst = (k - 1) % 2, k % 2

        def body(l, c, src=src, dst=dst):
            t_s[dst, l] = relax(src, l)
            return c

        lax.fori_loop(k, ze - k, body, 0)

    last = (SWEEPS - 1) % 2

    def final(i, c):
        new = relax(last, HALO + i)
        out_ref[i] = new[PAD_Y:PAD_Y + strip].T
        return c

    lax.fori_loop(0, local_depth, final, 0)


def local_body(temp_old, material, conduct_table, capacity_table, dyn_power, leak_ref, die_layer):
    temp_start = temp_old[:, 0]
    cells_mat = material[:, 0]
    local_depth, nx, strip = temp_start.shape
    depth_n = lax.axis_size("depth")
    lat_n = lax.axis_size("lat")
    dies = dyn_power.shape[0] * depth_n
    nz = local_depth * depth_n
    g = lax.axis_index("depth")
    s = lax.axis_index("lat")
    first_layer = g * local_depth
    ye = PAD_Y + strip + HALO + (-(PAD_Y + strip + HALO)) % 8

    xb = from_behind(jnp.stack([temp_start[local_depth - HALO:],
                                cells_mat[local_depth - HALO:].astype(jnp.float32)]), "depth", 1)
    xa = from_behind(jnp.stack([temp_start[:HALO], cells_mat[:HALO].astype(jnp.float32)]), "depth", -1)

    def cols(sl):
        parts = [temp_start[:, :, sl], cells_mat[:, :, sl].astype(jnp.float32),
                 dyn_power[:, 0, :, sl], leak_ref[:, 0, :, sl]]
        return jnp.transpose(jnp.concatenate(parts), (0, 2, 1))

    nf = 2 * local_depth + 2
    ylo = from_behind(cols(slice(strip - HALO, strip)), "lat", 1)
    yhi = from_behind(cols(slice(0, HALO)), "lat", -1)

    def widen(centre, lo, hi):
        return jnp.concatenate([jnp.zeros((PAD_Y - HALO, nx), jnp.float32), lo, centre, hi,
                                jnp.zeros((ye - (PAD_Y + strip + HALO), nx), jnp.float32)])

    side = jnp.concatenate([ylo[:2 * local_depth].reshape(2, local_depth, HALO, nx),
                            yhi[:2 * local_depth].reshape(2, local_depth, HALO, nx)], axis=2)
    cb = from_behind(side[:, local_depth - HALO:], "depth", 1)
    ca = from_behind(side[:, :HALO], "depth", -1)

    def pick(die):
        at = die_layer[die] - first_layer
        atc = jnp.clip(at, 0, local_depth - 1)
        layer = widen(lax.dynamic_index_in_dim(temp_start, atc, 0, keepdims=False).T,
                      lax.dynamic_index_in_dim(ylo, atc, 0, keepdims=False),
                      lax.dynamic_index_in_dim(yhi, atc, 0, keepdims=False))
        return jnp.where((at >= 0) & (at < local_depth), layer, 0.0)

    die_temp = pick(g)
    for o in range(1, dies):
        route = [(i, (i + o) % depth_n) for i in range(depth_n)]
        die_temp = die_temp + lax.ppermute(pick((g + o) % dies), "depth", route)
    dyn_w = widen(dyn_power[0, 0].T, ylo[nf - 2], yhi[nf - 2])
    leak_w = widen(leak_ref[0, 0].T, ylo[nf - 1], yhi[nf - 1])
    power_w = dyn_w + leak_w * jnp.exp(LEAK_SLOPE * die_temp)
    die_power = power_w[PAD_Y:PAD_Y + strip].T[None]

    slots = [power_w]
    for o in range(1, dies):
        route = [(i, (i + o) % depth_n) for i in range(depth_n)]
        slots.append(lax.ppermute(power_w, "depth", route))

    sc = jnp.concatenate([jnp.stack([g, s]).astype(jnp.int32), die_layer.astype(jnp.int32)])
    ze = local_depth + 2 * HALO
    smem = pl.BlockSpec(memory_space=pltpu.MemorySpace.SMEM)
    vmem = pl.BlockSpec(memory_space=pltpu.MemorySpace.VMEM)
    full = (ze, ye, nx)
    kern = functools.partial(sweep_kernel, nz, strip * lat_n, local_depth, strip)
    out = pl.pallas_call(
        kern,
        out_shape=jax.ShapeDtypeStruct((local_depth, nx, strip), jnp.float32),
        in_specs=[smem] * 3 + [vmem] * 12,
        out_specs=vmem,
        scratch_shapes=([pltpu.VMEM((2,) + full, jnp.float32)] + [pltpu.VMEM(full, jnp.float32)] * 8),
        compiler_params=pltpu.CompilerParams(vmem_limit_bytes=60 * 1024 * 1024),
        interpret=INTERPRET,
    )(sc, conduct_table, capacity_table, temp_start, cells_mat, xb, xa, ylo, yhi, cb, ca, *slots)
    return (out[:, None], die_power[:, None])


def solution(mesh):
    return jax.shard_map(
        local_body,
        mesh=mesh,
        in_specs=(
            P("depth", "lat", None, None),
            P("depth", "lat", None, None),
            P(),
            P(),
            P("depth", "lat", None, None),
            P("depth", "lat", None, None),
            P(),
        ),
        out_specs=(P("depth", "lat", None, None), P("depth", "lat", None, None)),
        check_vma=False,
    )
```

```python
import functools

import jax
import jax.numpy as jnp
from jax import lax
from jax.experimental import pallas as pl
from jax.experimental.pallas import tpu as pltpu
from jax.sharding import PartitionSpec as P


SWEEPS = 6
HALO = SWEEPS
PAD_Y = 8

COND_SLOPE = 0.15
LEAK_SLOPE = 0.5
SINK_CONDUCT = 2.0

INTERPRET = False


def from_behind(block, axis, distance):
    devices = range(lax.axis_size(axis))
    route = [(i - distance, i) for i in devices if i - distance in devices]
    return lax.ppermute(block, axis, route)


def harm(a, b):
    summed = a + b
    return 2.0 * a * b / jnp.where(summed > 0, summed, 1.0)


def material_bits(material):
    hi = material >= 4.0
    rest = material - jnp.where(hi, 4.0, 0.0)
    mid = rest >= 2.0
    lo = (rest - jnp.where(mid, 2.0, 0.0)) >= 1.0
    return hi, mid, lo


def lookup(table_ref, bits):
    hi, mid, lo = bits
    t = [table_ref[i] for i in range(8)]
    low = jnp.where(mid, jnp.where(lo, t[3], t[2]), jnp.where(lo, t[1], t[0]))
    high = jnp.where(mid, jnp.where(lo, t[7], t[6]), jnp.where(lo, t[5], t[4]))
    return jnp.where(hi, high, low)


def sweep_kernel(nz, ny_total, local_depth, strip,
                 sc_ref, ctab_ref, htab_ref, tc_ref, mc_ref, xb_ref, xa_ref,
                 ylo_ref, yhi_ref, cb_ref, ca_ref, d0_ref, d1_ref, d2_ref, d3_ref,
                 out_ref, t_s, cond_s, rhs_s, inv_s, gz_s, gx_s, gxl_s, gy_s, gyu_s):
    ze = t_s.shape[1]
    ye = t_s.shape[2]
    xe = t_s.shape[3]
    g = sc_ref[0]
    s = sc_ref[1]
    z0 = g * local_depth - HALO
    row = lax.broadcasted_iota(jnp.int32, (ye, xe), 0)
    lane = lax.broadcasted_iota(jnp.int32, (ye, xe), 1)
    yg = s * strip + row - PAD_Y
    yvalid = (yg >= 0) & (yg < ny_total) & (row >= PAD_Y - HALO) & (row < PAD_Y + strip + HALO)
    top = PAD_Y + strip + HALO
    zlo = jnp.zeros((PAD_Y - HALO, xe), jnp.float32)
    zhi = jnp.zeros((ye - top, xe), jnp.float32)

    def put(dst, centre, lo, hi):
        dst[PAD_Y - HALO:PAD_Y] = lo
        dst[PAD_Y:PAD_Y + strip] = centre
        dst[PAD_Y + strip:top] = hi
        dst[0:PAD_Y - HALO] = zlo
        dst[top:ye] = zhi

    def tables(l, temp_raw, mat_raw, t_lo, t_hi, m_lo, m_hi):
        put(t_s.at[0, l], temp_raw.T, t_lo, t_hi)
        put(cond_s.at[l], mat_raw.T.astype(jnp.float32), m_lo, m_hi)
        temp = t_s[0, l]
        mat = cond_s[l]
        zg = z0 + l
        valid = yvalid & (zg >= 0) & (zg < nz)
        bits = material_bits(mat)
        cval = lookup(ctab_ref, bits)
        hval = lookup(htab_ref, bits)
        cond = jnp.where(valid, cval * jnp.exp(-COND_SLOPE * temp), 0.0)
        cond_s[l] = cond
        inv_s[l] = hval
        rhs_s[l] = hval * temp

    def below(i, c):
        tables(i, xb_ref[0, i], xb_ref[1, i], cb_ref[0, i, :HALO], cb_ref[0, i, HALO:],
               cb_ref[1, i, :HALO], cb_ref[1, i, HALO:])
        return c

    def centre(i, c):
        tables(HALO + i, tc_ref[i], mc_ref[i], ylo_ref[i], yhi_ref[i],
               ylo_ref[local_depth + i], yhi_ref[local_depth + i])
        return c

    def above(i, c):
        tables(HALO + local_depth + i, xa_ref[0, i], xa_ref[1, i], ca_ref[0, i, :HALO], ca_ref[0, i, HALO:],
               ca_ref[1, i, :HALO], ca_ref[1, i, HALO:])
        return c

    lax.fori_loop(0, HALO, below, 0)
    lax.fori_loop(0, local_depth, centre, 0)
    lax.fori_loop(0, HALO, above, 0)

    slots = (d0_ref, d1_ref, d2_ref, d3_ref)
    dies = len(slots)
    for o in range(dies):
        rel = sc_ref[2 + (g + dies - o) % dies] - z0
        relc = jnp.clip(rel, 0, ze - 1)

        @pl.when((rel >= 0) & (rel < ze))
        def _():
            rhs_s[relc] = inv_s[relc] * t_s[0, relc] + slots[o][...]

    def faces_z(l, c):
        gz_s[l] = harm(cond_s[l], cond_s[l + 1])
        return c

    lax.fori_loop(0, ze - 1, faces_z, 0)
    gz_s[ze - 1] = jnp.zeros((ye, xe), jnp.float32)

    def faces(l, c):
        cc = cond_s[l]
        gx = harm(cc, pltpu.roll(cc, xe - 1, 1))
        gx = jnp.where(lane == xe - 1, 0.0, gx)
        gy = harm(cc, pltpu.roll(cc, ye - 1, 0))
        gy = jnp.where(row == ye - 1, 0.0, gy)
        gxl = pltpu.roll(gx, 1, 1)
        gyu = pltpu.roll(gy, 1, 0)
        gx_s[l] = gx
        gxl_s[l] = gxl
        gy_s[l] = gy
        gyu_s[l] = gyu
        lm = jnp.maximum(l - 1, 0)
        gzm = jnp.where(l > 0, gz_s[lm], 0.0)
        sink = jnp.where(z0 + l == 0, SINK_CONDUCT, 0.0)
        diag = inv_s[l] + (gz_s[l] + gzm + gx + gxl + gy + gyu) + sink
        inv_s[l] = 1.0 / diag
        return c

    lax.fori_loop(1, ze - 1, faces, 0)

    def relax(src, l):
        t = t_s[src, l]
        coupled = (gz_s[l] * t_s[src, l + 1] + gz_s[l - 1] * t_s[src, l - 1]
                   + gx_s[l] * pltpu.roll(t, xe - 1, 1) + gxl_s[l] * pltpu.roll(t, 1, 1)
                   + gy_s[l] * pltpu.roll(t, ye - 1, 0) + gyu_s[l] * pltpu.roll(t, 1, 0))
        return (rhs_s[l] + coupled) * inv_s[l]

    for k in range(1, SWEEPS):
        src, dst = (k - 1) % 2, k % 2

        def body(l, c, src=src, dst=dst):
            t_s[dst, l] = relax(src, l)
            return c

        lax.fori_loop(k, ze - k, body, 0)

    last = (SWEEPS - 1) % 2

    def final(i, c):
        new = relax(last, HALO + i)
        out_ref[i] = new[PAD_Y:PAD_Y + strip].T
        return c

    lax.fori_loop(0, local_depth, final, 0)


def local_body(temp_old, material, conduct_table, capacity_table, dyn_power, leak_ref, die_layer):
    temp_start = temp_old[:, 0]
    cells_mat = material[:, 0]
    local_depth, nx, strip = temp_start.shape
    depth_n = lax.axis_size("depth")
    lat_n = lax.axis_size("lat")
    dies = dyn_power.shape[0] * depth_n
    nz = local_depth * depth_n
    g = lax.axis_index("depth")
    s = lax.axis_index("lat")
    first_layer = g * local_depth
    ye = PAD_Y + strip + HALO + (-(PAD_Y + strip + HALO)) % 8

    xb = from_behind(jnp.stack([temp_start[local_depth - HALO:],
                                cells_mat[local_depth - HALO:].astype(jnp.float32)]), "depth", 1)
    xa = from_behind(jnp.stack([temp_start[:HALO], cells_mat[:HALO].astype(jnp.float32)]), "depth", -1)

    def cols(sl):
        parts = [temp_start[:, :, sl], cells_mat[:, :, sl].astype(jnp.float32),
                 dyn_power[:, 0, :, sl], leak_ref[:, 0, :, sl]]
        return jnp.transpose(jnp.concatenate(parts), (0, 2, 1))

    nf = 2 * local_depth + 2
    ylo = from_behind(cols(slice(strip - HALO, strip)), "lat", 1)
    yhi = from_behind(cols(slice(0, HALO)), "lat", -1)

    def widen(centre, lo, hi):
        return jnp.concatenate([jnp.zeros((PAD_Y - HALO, nx), jnp.float32), lo, centre, hi,
                                jnp.zeros((ye - (PAD_Y + strip + HALO), nx), jnp.float32)])

    side = jnp.concatenate([ylo[:2 * local_depth].reshape(2, local_depth, HALO, nx),
                            yhi[:2 * local_depth].reshape(2, local_depth, HALO, nx)], axis=2)
    corner_of = {1: side[:, local_depth - HALO:], dies - 1: side[:, :HALO]}

    def pick(die):
        at = die_layer[die] - first_layer
        atc = jnp.clip(at, 0, local_depth - 1)
        layer = widen(lax.dynamic_index_in_dim(temp_start, atc, 0, keepdims=False).T,
                      lax.dynamic_index_in_dim(ylo, atc, 0, keepdims=False),
                      lax.dynamic_index_in_dim(yhi, atc, 0, keepdims=False))
        return jnp.where((at >= 0) & (at < local_depth), layer, 0.0)

    die_temp = pick(g)
    got_corners = {}
    for o in range(1, dies):
        route = [(i, (i + o) % depth_n) for i in range(depth_n)]
        sent = pick((g + o) % dies)
        if o in corner_of:
            sent = jnp.concatenate([sent, corner_of[o].reshape(-1, nx)])
        got = lax.ppermute(sent, "depth", route)
        die_temp = die_temp + got[:ye]
        if o in corner_of:
            got_corners[o] = got[ye:].reshape(2, HALO, 2 * HALO, nx)
    cb, ca = got_corners[1], got_corners[dies - 1]
    dyn_w = widen(dyn_power[0, 0].T, ylo[nf - 2], yhi[nf - 2])
    leak_w = widen(leak_ref[0, 0].T, ylo[nf - 1], yhi[nf - 1])
    power_w = dyn_w + leak_w * jnp.exp(LEAK_SLOPE * die_temp)
    die_power = power_w[PAD_Y:PAD_Y + strip].T[None]

    slots = [power_w]
    for o in range(1, dies):
        route = [(i, (i + o) % depth_n) for i in range(depth_n)]
        slots.append(lax.ppermute(power_w, "depth", route))

    sc = jnp.concatenate([jnp.stack([g, s]).astype(jnp.int32), die_layer.astype(jnp.int32)])
    ze = local_depth + 2 * HALO
    smem = pl.BlockSpec(memory_space=pltpu.MemorySpace.SMEM)
    vmem = pl.BlockSpec(memory_space=pltpu.MemorySpace.VMEM)
    full = (ze, ye, nx)
    kern = functools.partial(sweep_kernel, nz, strip * lat_n, local_depth, strip)
    out = pl.pallas_call(
        kern,
        out_shape=jax.ShapeDtypeStruct((local_depth, nx, strip), jnp.float32),
        in_specs=[smem] * 3 + [vmem] * 12,
        out_specs=vmem,
        scratch_shapes=([pltpu.VMEM((2,) + full, jnp.float32)] + [pltpu.VMEM(full, jnp.float32)] * 8),
        compiler_params=pltpu.CompilerParams(vmem_limit_bytes=60 * 1024 * 1024),
        interpret=INTERPRET,
    )(sc, conduct_table, capacity_table, temp_start, cells_mat, xb, xa, ylo, yhi, cb, ca, *slots)
    return (out[:, None], die_power[:, None])


def solution(mesh):
    return jax.shard_map(
        local_body,
        mesh=mesh,
        in_specs=(
            P("depth", "lat", None, None),
            P("depth", "lat", None, None),
            P(),
            P(),
            P("depth", "lat", None, None),
            P("depth", "lat", None, None),
            P(),
        ),
        out_specs=(P("depth", "lat", None, None), P("depth", "lat", None, None)),
        check_vma=False,
    )
```

```python
import functools

import jax
import jax.numpy as jnp
from jax import lax
from jax.experimental import pallas as pl
from jax.experimental.pallas import tpu as pltpu
from jax.sharding import PartitionSpec as P


SWEEPS = 6
HALO = SWEEPS
PAD_Y = 8

COND_SLOPE = 0.15
LEAK_SLOPE = 0.5
SINK_CONDUCT = 2.0

INTERPRET = False


def from_behind(block, axis, distance):
    devices = range(lax.axis_size(axis))
    route = [(i - distance, i) for i in devices if i - distance in devices]
    return lax.ppermute(block, axis, route)


def harm(a, b):
    summed = a + b
    return 2.0 * a * b / jnp.where(summed > 0, summed, 1.0)


def material_bits(material):
    hi = material >= 4.0
    rest = material - jnp.where(hi, 4.0, 0.0)
    mid = rest >= 2.0
    lo = (rest - jnp.where(mid, 2.0, 0.0)) >= 1.0
    return hi, mid, lo


def lookup(table_ref, bits):
    hi, mid, lo = bits
    t = [table_ref[i] for i in range(8)]
    low = jnp.where(mid, jnp.where(lo, t[3], t[2]), jnp.where(lo, t[1], t[0]))
    high = jnp.where(mid, jnp.where(lo, t[7], t[6]), jnp.where(lo, t[5], t[4]))
    return jnp.where(hi, high, low)


def sweep_kernel(nz, ny_total, local_depth, strip,
                 sc_ref, ctab_ref, htab_ref, tc_ref, mc_ref, xb_ref, xa_ref,
                 ylo_ref, yhi_ref, cb_ref, ca_ref, d0_ref, d1_ref, d2_ref, d3_ref,
                 out_ref, t_s, cond_s, rhs_s, inv_s, gz_s, gx_s, gxl_s, gy_s, gyu_s):
    ze = t_s.shape[1]
    ye = t_s.shape[2]
    xe = t_s.shape[3]
    g = sc_ref[0]
    s = sc_ref[1]
    z0 = g * local_depth - HALO
    row = lax.broadcasted_iota(jnp.int32, (ye, xe), 0)
    lane = lax.broadcasted_iota(jnp.int32, (ye, xe), 1)
    yg = s * strip + row - PAD_Y
    yvalid = (yg >= 0) & (yg < ny_total) & (row >= PAD_Y - HALO) & (row < PAD_Y + strip + HALO)
    top = PAD_Y + strip + HALO
    zlo = jnp.zeros((PAD_Y - HALO, xe), jnp.float32)
    zhi = jnp.zeros((ye - top, xe), jnp.float32)

    def put(dst, centre, lo, hi):
        dst[PAD_Y - HALO:PAD_Y] = lo
        dst[PAD_Y:PAD_Y + strip] = centre
        dst[PAD_Y + strip:top] = hi
        dst[0:PAD_Y - HALO] = zlo
        dst[top:ye] = zhi

    def tables(l, temp_raw, mat_raw, t_lo, t_hi, m_lo, m_hi):
        put(t_s.at[0, l], temp_raw.T, t_lo, t_hi)
        put(cond_s.at[l], mat_raw.T.astype(jnp.float32), m_lo, m_hi)
        temp = t_s[0, l]
        mat = cond_s[l]
        zg = z0 + l
        valid = yvalid & (zg >= 0) & (zg < nz)
        bits = material_bits(mat)
        cval = lookup(ctab_ref, bits)
        hval = lookup(htab_ref, bits)
        cond = jnp.where(valid, cval * jnp.exp(-COND_SLOPE * temp), 0.0)
        cond_s[l] = cond
        inv_s[l] = hval
        rhs_s[l] = hval * temp

    def below(i, c):
        tables(i, xb_ref[0, i], xb_ref[1, i], cb_ref[0, i, :HALO], cb_ref[0, i, HALO:],
               cb_ref[1, i, :HALO], cb_ref[1, i, HALO:])
        return c

    def centre(i, c):
        tables(HALO + i, tc_ref[i], mc_ref[i], ylo_ref[i], yhi_ref[i],
               ylo_ref[local_depth + i], yhi_ref[local_depth + i])
        return c

    def above(i, c):
        tables(HALO + local_depth + i, xa_ref[0, i], xa_ref[1, i], ca_ref[0, i, :HALO], ca_ref[0, i, HALO:],
               ca_ref[1, i, :HALO], ca_ref[1, i, HALO:])
        return c

    lax.fori_loop(0, HALO, below, 0)
    lax.fori_loop(0, local_depth, centre, 0)
    lax.fori_loop(0, HALO, above, 0)

    slots = (d0_ref, d1_ref, d2_ref, d3_ref)
    dies = len(slots)
    for o in range(dies):
        rel = sc_ref[2 + (g + dies - o) % dies] - z0
        relc = jnp.clip(rel, 0, ze - 1)

        @pl.when((rel >= 0) & (rel < ze))
        def _():
            rhs_s[relc] = inv_s[relc] * t_s[0, relc] + slots[o][...]

    gz_s[0] = harm(cond_s[0], cond_s[1])

    def faces(l, c):
        cc = cond_s[l]
        gzp = harm(cc, cond_s[l + 1])
        gz_s[l] = gzp
        gx = harm(cc, pltpu.roll(cc, xe - 1, 1))
        gx = jnp.where(lane == xe - 1, 0.0, gx)
        gy = harm(cc, pltpu.roll(cc, ye - 1, 0))
        gy = jnp.where(row == ye - 1, 0.0, gy)
        gxl = pltpu.roll(gx, 1, 1)
        gyu = pltpu.roll(gy, 1, 0)
        gx_s[l] = gx
        gxl_s[l] = gxl
        gy_s[l] = gy
        gyu_s[l] = gyu
        sink = jnp.where(z0 + l == 0, SINK_CONDUCT, 0.0)
        diag = inv_s[l] + (gzp + gz_s[l - 1] + gx + gxl + gy + gyu) + sink
        inv_s[l] = 1.0 / diag
        return c

    lax.fori_loop(1, ze - 1, faces, 0)

    def relax(src, l):
        t = t_s[src, l]
        coupled = (gz_s[l] * t_s[src, l + 1] + gz_s[l - 1] * t_s[src, l - 1]
                   + gx_s[l] * pltpu.roll(t, xe - 1, 1) + gxl_s[l] * pltpu.roll(t, 1, 1)
                   + gy_s[l] * pltpu.roll(t, ye - 1, 0) + gyu_s[l] * pltpu.roll(t, 1, 0))
        return (rhs_s[l] + coupled) * inv_s[l]

    for k in range(1, SWEEPS):
        src, dst = (k - 1) % 2, k % 2

        def body(l, c, src=src, dst=dst):
            t_s[dst, l] = relax(src, l)
            return c

        lax.fori_loop(k, ze - k, body, 0)

    last = (SWEEPS - 1) % 2

    def final(i, c):
        new = relax(last, HALO + i)
        out_ref[i] = new[PAD_Y:PAD_Y + strip].T
        return c

    lax.fori_loop(0, local_depth, final, 0)


def local_body(temp_old, material, conduct_table, capacity_table, dyn_power, leak_ref, die_layer):
    temp_start = temp_old[:, 0]
    cells_mat = material[:, 0]
    local_depth, nx, strip = temp_start.shape
    depth_n = lax.axis_size("depth")
    lat_n = lax.axis_size("lat")
    dies = dyn_power.shape[0] * depth_n
    nz = local_depth * depth_n
    g = lax.axis_index("depth")
    s = lax.axis_index("lat")
    first_layer = g * local_depth
    ye = PAD_Y + strip + HALO + (-(PAD_Y + strip + HALO)) % 8

    xb = from_behind(jnp.stack([temp_start[local_depth - HALO:],
                                cells_mat[local_depth - HALO:].astype(jnp.float32)]), "depth", 1)
    xa = from_behind(jnp.stack([temp_start[:HALO], cells_mat[:HALO].astype(jnp.float32)]), "depth", -1)

    def cols(sl):
        parts = [temp_start[:, :, sl], cells_mat[:, :, sl].astype(jnp.float32),
                 dyn_power[:, 0, :, sl], leak_ref[:, 0, :, sl]]
        return jnp.transpose(jnp.concatenate(parts), (0, 2, 1))

    nf = 2 * local_depth + 2
    ylo = from_behind(cols(slice(strip - HALO, strip)), "lat", 1)
    yhi = from_behind(cols(slice(0, HALO)), "lat", -1)

    def widen(centre, lo, hi):
        return jnp.concatenate([jnp.zeros((PAD_Y - HALO, nx), jnp.float32), lo, centre, hi,
                                jnp.zeros((ye - (PAD_Y + strip + HALO), nx), jnp.float32)])

    side = jnp.concatenate([ylo[:2 * local_depth].reshape(2, local_depth, HALO, nx),
                            yhi[:2 * local_depth].reshape(2, local_depth, HALO, nx)], axis=2)
    cb = from_behind(side[:, local_depth - HALO:], "depth", 1)
    ca = from_behind(side[:, :HALO], "depth", -1)

    def pick(die):
        at = die_layer[die] - first_layer
        atc = jnp.clip(at, 0, local_depth - 1)
        layer = widen(lax.dynamic_index_in_dim(temp_start, atc, 0, keepdims=False).T,
                      lax.dynamic_index_in_dim(ylo, atc, 0, keepdims=False),
                      lax.dynamic_index_in_dim(yhi, atc, 0, keepdims=False))
        return jnp.where((at >= 0) & (at < local_depth), layer, 0.0)

    die_temp = pick(g)
    for o in range(1, dies):
        route = [(i, (i + o) % depth_n) for i in range(depth_n)]
        die_temp = die_temp + lax.ppermute(pick((g + o) % dies), "depth", route)
    dyn_w = widen(dyn_power[0, 0].T, ylo[nf - 2], yhi[nf - 2])
    leak_w = widen(leak_ref[0, 0].T, ylo[nf - 1], yhi[nf - 1])
    power_w = dyn_w + leak_w * jnp.exp(LEAK_SLOPE * die_temp)
    die_power = power_w[PAD_Y:PAD_Y + strip].T[None]

    slots = [power_w]
    for o in range(1, dies):
        route = [(i, (i + o) % depth_n) for i in range(depth_n)]
        slots.append(lax.ppermute(power_w, "depth", route))

    sc = jnp.concatenate([jnp.stack([g, s]).astype(jnp.int32), die_layer.astype(jnp.int32)])
    ze = local_depth + 2 * HALO
    smem = pl.BlockSpec(memory_space=pltpu.MemorySpace.SMEM)
    vmem = pl.BlockSpec(memory_space=pltpu.MemorySpace.VMEM)
    full = (ze, ye, nx)
    kern = functools.partial(sweep_kernel, nz, strip * lat_n, local_depth, strip)
    out = pl.pallas_call(
        kern,
        out_shape=jax.ShapeDtypeStruct((local_depth, nx, strip), jnp.float32),
        in_specs=[smem] * 3 + [vmem] * 12,
        out_specs=vmem,
        scratch_shapes=([pltpu.VMEM((2,) + full, jnp.float32)] + [pltpu.VMEM(full, jnp.float32)] * 8),
        compiler_params=pltpu.CompilerParams(vmem_limit_bytes=60 * 1024 * 1024),
        interpret=INTERPRET,
    )(sc, conduct_table, capacity_table, temp_start, cells_mat, xb, xa, ylo, yhi, cb, ca, *slots)
    return (out[:, None], die_power[:, None])


def solution(mesh):
    return jax.shard_map(
        local_body,
        mesh=mesh,
        in_specs=(
            P("depth", "lat", None, None),
            P("depth", "lat", None, None),
            P(),
            P(),
            P("depth", "lat", None, None),
            P("depth", "lat", None, None),
            P(),
        ),
        out_specs=(P("depth", "lat", None, None), P("depth", "lat", None, None)),
        check_vma=False,
    )
```

```python
import functools

import jax
import jax.numpy as jnp
from jax import lax
from jax.experimental import pallas as pl
from jax.experimental.pallas import tpu as pltpu
from jax.sharding import PartitionSpec as P


SWEEPS = 6
HALO = SWEEPS
PAD_Y = 8

COND_SLOPE = 0.15
LEAK_SLOPE = 0.5
SINK_CONDUCT = 2.0

INTERPRET = False


def from_behind(block, axis, distance):
    devices = range(lax.axis_size(axis))
    route = [(i - distance, i) for i in devices if i - distance in devices]
    return lax.ppermute(block, axis, route)


def harm(a, b):
    summed = a + b
    return 2.0 * a * b / jnp.where(summed > 0, summed, 1.0)


def material_bits(material):
    hi = material >= 4.0
    rest = material - jnp.where(hi, 4.0, 0.0)
    mid = rest >= 2.0
    lo = (rest - jnp.where(mid, 2.0, 0.0)) >= 1.0
    return hi, mid, lo


def lookup(table_ref, bits):
    hi, mid, lo = bits
    t = [table_ref[i] for i in range(8)]
    low = jnp.where(mid, jnp.where(lo, t[3], t[2]), jnp.where(lo, t[1], t[0]))
    high = jnp.where(mid, jnp.where(lo, t[7], t[6]), jnp.where(lo, t[5], t[4]))
    return jnp.where(hi, high, low)


def sweep_kernel(nz, ny_total, local_depth, strip,
                 sc_ref, ctab_ref, htab_ref, tc_ref, mc_ref, xb_ref, xa_ref,
                 ylo_ref, yhi_ref, cb_ref, ca_ref, d0_ref, d1_ref, d2_ref, d3_ref,
                 out_ref, t_s, cond_s, rhs_s, inv_s, gz_s, gx_s, gxl_s, gy_s, gyu_s):
    ze = t_s.shape[1]
    ye = t_s.shape[2]
    xe = t_s.shape[3]
    g = sc_ref[0]
    s = sc_ref[1]
    z0 = g * local_depth - HALO
    row = lax.broadcasted_iota(jnp.int32, (ye, xe), 0)
    lane = lax.broadcasted_iota(jnp.int32, (ye, xe), 1)
    yg = s * strip + row - PAD_Y
    yvalid = (yg >= 0) & (yg < ny_total) & (row >= PAD_Y - HALO) & (row < PAD_Y + strip + HALO)
    top = PAD_Y + strip + HALO
    zlo = jnp.zeros((PAD_Y - HALO, xe), jnp.float32)
    zhi = jnp.zeros((ye - top, xe), jnp.float32)

    def put(dst, centre, lo, hi):
        dst[PAD_Y - HALO:PAD_Y] = lo
        dst[PAD_Y:PAD_Y + strip] = centre
        dst[PAD_Y + strip:top] = hi
        dst[0:PAD_Y - HALO] = zlo
        dst[top:ye] = zhi

    def tables(l, temp_raw, mat_raw, t_lo, t_hi, m_lo, m_hi):
        put(t_s.at[0, l], temp_raw.T, t_lo, t_hi)
        put(cond_s.at[l], mat_raw.T.astype(jnp.float32), m_lo, m_hi)
        temp = t_s[0, l]
        mat = cond_s[l]
        zg = z0 + l
        valid = yvalid & (zg >= 0) & (zg < nz)
        bits = material_bits(mat)
        cval = lookup(ctab_ref, bits)
        hval = lookup(htab_ref, bits)
        cond = jnp.where(valid, cval * jnp.exp(-COND_SLOPE * temp), 0.0)
        cond_s[l] = cond
        inv_s[l] = hval
        rhs_s[l] = hval * temp

    def below(i, c):
        tables(i, xb_ref[0, i], xb_ref[1, i], cb_ref[0, i, :HALO], cb_ref[0, i, HALO:],
               cb_ref[1, i, :HALO], cb_ref[1, i, HALO:])
        return c

    def centre(i, c):
        tables(HALO + i, tc_ref[i], mc_ref[i], ylo_ref[i], yhi_ref[i],
               ylo_ref[local_depth + i], yhi_ref[local_depth + i])
        return c

    def above(i, c):
        tables(HALO + local_depth + i, xa_ref[0, i], xa_ref[1, i], ca_ref[0, i, :HALO], ca_ref[0, i, HALO:],
               ca_ref[1, i, :HALO], ca_ref[1, i, HALO:])
        return c

    lax.fori_loop(0, HALO, below, 0)
    lax.fori_loop(0, local_depth, centre, 0)
    lax.fori_loop(0, HALO, above, 0)

    slots = (d0_ref, d1_ref, d2_ref, d3_ref)
    dies = len(slots)
    for o in range(dies):
        rel = sc_ref[2 + (g + dies - o) % dies] - z0
        relc = jnp.clip(rel, 0, ze - 1)

        @pl.when((rel >= 0) & (rel < ze))
        def _():
            rhs_s[relc] = inv_s[relc] * t_s[0, relc] + slots[o][...]

    gz_s[0] = harm(cond_s[0], cond_s[1])

    def faces(l, c):
        cc = cond_s[l]
        gzp = harm(cc, cond_s[l + 1])
        gz_s[l] = gzp
        gx = harm(cc, pltpu.roll(cc, xe - 1, 1))
        gx = jnp.where(lane == xe - 1, 0.0, gx)
        gy = harm(cc, pltpu.roll(cc, ye - 1, 0))
        gxl = pltpu.roll(gx, 1, 1)
        gyu = pltpu.roll(gy, 1, 0)
        gx_s[l] = gx
        gxl_s[l] = gxl
        gy_s[l] = gy
        gyu_s[l] = gyu
        sink = jnp.where(z0 + l == 0, SINK_CONDUCT, 0.0)
        diag = inv_s[l] + (gzp + gz_s[l - 1] + gx + gxl + gy + gyu) + sink
        inv_s[l] = 1.0 / diag
        return c

    lax.fori_loop(1, ze - 1, faces, 0)

    def relax(src, l):
        t = t_s[src, l]
        coupled = (gz_s[l] * t_s[src, l + 1] + gz_s[l - 1] * t_s[src, l - 1]
                   + gx_s[l] * pltpu.roll(t, xe - 1, 1) + gxl_s[l] * pltpu.roll(t, 1, 1)
                   + gy_s[l] * pltpu.roll(t, ye - 1, 0) + gyu_s[l] * pltpu.roll(t, 1, 0))
        return (rhs_s[l] + coupled) * inv_s[l]

    for k in range(1, SWEEPS):
        src, dst = (k - 1) % 2, k % 2

        def body(l, c, src=src, dst=dst):
            t_s[dst, l] = relax(src, l)
            return c

        lax.fori_loop(k, ze - k, body, 0, unroll=2)

    last = (SWEEPS - 1) % 2

    def final(i, c):
        new = relax(last, HALO + i)
        out_ref[i] = new[PAD_Y:PAD_Y + strip].T
        return c

    lax.fori_loop(0, local_depth, final, 0, unroll=2)


def local_body(temp_old, material, conduct_table, capacity_table, dyn_power, leak_ref, die_layer):
    temp_start = temp_old[:, 0]
    cells_mat = material[:, 0]
    local_depth, nx, strip = temp_start.shape
    depth_n = lax.axis_size("depth")
    lat_n = lax.axis_size("lat")
    dies = dyn_power.shape[0] * depth_n
    nz = local_depth * depth_n
    g = lax.axis_index("depth")
    s = lax.axis_index("lat")
    first_layer = g * local_depth
    ye = PAD_Y + strip + HALO + (-(PAD_Y + strip + HALO)) % 8

    xb = from_behind(jnp.stack([temp_start[local_depth - HALO:],
                                cells_mat[local_depth - HALO:].astype(jnp.float32)]), "depth", 1)
    xa = from_behind(jnp.stack([temp_start[:HALO], cells_mat[:HALO].astype(jnp.float32)]), "depth", -1)

    def cols(sl):
        parts = [temp_start[:, :, sl], cells_mat[:, :, sl].astype(jnp.float32),
                 dyn_power[:, 0, :, sl], leak_ref[:, 0, :, sl]]
        return jnp.transpose(jnp.concatenate(parts), (0, 2, 1))

    nf = 2 * local_depth + 2
    ylo = from_behind(cols(slice(strip - HALO, strip)), "lat", 1)
    yhi = from_behind(cols(slice(0, HALO)), "lat", -1)

    def widen(centre, lo, hi):
        return jnp.concatenate([jnp.zeros((PAD_Y - HALO, nx), jnp.float32), lo, centre, hi,
                                jnp.zeros((ye - (PAD_Y + strip + HALO), nx), jnp.float32)])

    side = jnp.concatenate([ylo[:2 * local_depth].reshape(2, local_depth, HALO, nx),
                            yhi[:2 * local_depth].reshape(2, local_depth, HALO, nx)], axis=2)
    cb = from_behind(side[:, local_depth - HALO:], "depth", 1)
    ca = from_behind(side[:, :HALO], "depth", -1)

    def pick(die):
        at = die_layer[die] - first_layer
        atc = jnp.clip(at, 0, local_depth - 1)
        layer = widen(lax.dynamic_index_in_dim(temp_start, atc, 0, keepdims=False).T,
                      lax.dynamic_index_in_dim(ylo, atc, 0, keepdims=False),
                      lax.dynamic_index_in_dim(yhi, atc, 0, keepdims=False))
        return jnp.where((at >= 0) & (at < local_depth), layer, 0.0)

    die_temp = pick(g)
    for o in range(1, dies):
        route = [(i, (i + o) % depth_n) for i in range(depth_n)]
        die_temp = die_temp + lax.ppermute(pick((g + o) % dies), "depth", route)
    dyn_w = widen(dyn_power[0, 0].T, ylo[nf - 2], yhi[nf - 2])
    leak_w = widen(leak_ref[0, 0].T, ylo[nf - 1], yhi[nf - 1])
    power_w = dyn_w + leak_w * jnp.exp(LEAK_SLOPE * die_temp)
    die_power = power_w[PAD_Y:PAD_Y + strip].T[None]

    slots = [power_w]
    for o in range(1, dies):
        route = [(i, (i + o) % depth_n) for i in range(depth_n)]
        slots.append(lax.ppermute(power_w, "depth", route))

    sc = jnp.concatenate([jnp.stack([g, s]).astype(jnp.int32), die_layer.astype(jnp.int32)])
    ze = local_depth + 2 * HALO
    smem = pl.BlockSpec(memory_space=pltpu.MemorySpace.SMEM)
    vmem = pl.BlockSpec(memory_space=pltpu.MemorySpace.VMEM)
    full = (ze, ye, nx)
    kern = functools.partial(sweep_kernel, nz, strip * lat_n, local_depth, strip)
    out = pl.pallas_call(
        kern,
        out_shape=jax.ShapeDtypeStruct((local_depth, nx, strip), jnp.float32),
        in_specs=[smem] * 3 + [vmem] * 12,
        out_specs=vmem,
        scratch_shapes=([pltpu.VMEM((2,) + full, jnp.float32)] + [pltpu.VMEM(full, jnp.float32)] * 8),
        compiler_params=pltpu.CompilerParams(vmem_limit_bytes=60 * 1024 * 1024),
        interpret=INTERPRET,
    )(sc, conduct_table, capacity_table, temp_start, cells_mat, xb, xa, ylo, yhi, cb, ca, *slots)
    return (out[:, None], die_power[:, None])


def solution(mesh):
    return jax.shard_map(
        local_body,
        mesh=mesh,
        in_specs=(
            P("depth", "lat", None, None),
            P("depth", "lat", None, None),
            P(),
            P(),
            P("depth", "lat", None, None),
            P("depth", "lat", None, None),
            P(),
        ),
        out_specs=(P("depth", "lat", None, None), P("depth", "lat", None, None)),
        check_vma=False,
    )
```
